128 devices in a mesh: lon: 16 (over y_hi, z, core), lat: 8 (over y_lo, x).
Axes of the slice: x: 4, y: 4 (y_hi: 2, y_lo: 2; y = y_hi * 2 + y_lo), z: 4, core: 2. Of those that a mesh axis runs over, the one named last changes fastest.
Arguments:
- zonal_current: float32 [32, 512, 2048], P(None, 'lat', 'lon'), may hold values from -6 to 6
- meridional_current: float32 [32, 512, 2048], P(None, 'lat', 'lon'), may hold values from -6 to 6
- warmth_anomaly: float32 [32, 512, 2048], P(None, 'lat', 'lon'), may hold values from -6 to 6
- brine_anomaly: float32 [32, 512, 2048], P(None, 'lat', 'lon'), may hold values from -6 to 6
- marine_indicator: int32 [512, 2048], P('lat', 'lon'), may hold values 0 or 1
- retained_tile_indicator: int32 [32, 128], P('lat', 'lon'), may hold values 0 or 1
- seabed_thickness: float32 [512, 2048], P('lat', 'lon'), may hold values from 0.25 to 2.5
- elevation_pivot_entry: float32 [512, 2048], P('lat', 'lon'), may hold values from 0.1 to 1
Outputs:
- zonal_next: float32 [32, 512, 2048], P(None, 'lat', 'lon')
- meridional_next: float32 [32, 512, 2048], P(None, 'lat', 'lon')
- temperature_next: float32 [32, 512, 2048], P(None, 'lat', 'lon')
- salinity_next: float32 [32, 512, 2048], P(None, 'lat', 'lon')
- surface_pressure: float32 [512, 2048], P('lat', 'lon')
- pressure_residual: float32 [512, 2048], P('lat', 'lon')
The draws below stay inside these ranges and needn't reach their ends.
All inputs are finite; a program needn't handle non-finite values. No bound on the sum of `marine_indicator` or of `retained_tile_indicator` on one device may be relied on, other than what follows from the above.
Results may differ from the reference program's by a relative error of at most 0.0003.
Values sent between devices are 32-bit elements; how exact they have to be, the bound alone decides.
No kernel may reach another device: no remote copies, remote signals or barrier semaphores. Data moves between devices by JAX's collectives and lax.ppermute only.
A program may use at most 128 MiB of HBM per device.

```python
import math
import jax
import jax.numpy as jnp
from jax import lax

VERTICAL_TIERS = 32
BLK = 16
ITERS = 3
PARALLEL_POINTS = 2048
MERIDIAN_POINTS = 512
NBX = 128
NBY = 32


def set_ends(drawn, stream_key, low, top_value):
    shape = drawn.shape
    spot = [jax.random.randint(jax.random.fold_in(stream_key, axis), (), 0, shape[axis]) for axis in range(len(shape))]
    drawn = drawn.at[tuple(spot)].set(low)
    longest = shape.index(max(shape))
    spot[longest] = (spot[longest] + 1) % shape[longest]
    return drawn.at[tuple(spot)].set(top_value)


def shard_levels(own_key, dims, cuts, low, largest):
    loudness = 1.0
    for axis_at, blocks in cuts:
        heights = jax.random.uniform(jax.random.fold_in(jax.random.fold_in(own_key, 6), axis_at), (blocks,), jnp.float32, low / len(cuts), largest / len(cuts))
        loudness = loudness * jnp.repeat(jnp.exp(heights), dims[axis_at] // blocks).reshape((-1,) + (1,) * (len(dims) - 1 - axis_at))
    return loudness


def scatter_about(rng, dims, deviation, reach, pieces=(), kind=jnp.bfloat16):
    array = jax.random.normal(rng, dims, jnp.float32) * deviation
    if len(pieces) > 0:
        array = shard_levels(rng, dims, pieces, -0.22, 0.18) * array
    return jnp.clip(array, min=-reach, max=reach).astype(kind)


def setup_inputs(seed: int = 0) -> dict:
    streams_of = jax.random.split(jax.random.key(seed), 9)
    return {
        "zonal_current": scatter_about(streams_of[0], (VERTICAL_TIERS, MERIDIAN_POINTS, PARALLEL_POINTS), 1.0, 6.0, ((1, 8), (2, 16)), jnp.float32),
        "meridional_current": scatter_about(streams_of[1], (VERTICAL_TIERS, MERIDIAN_POINTS, PARALLEL_POINTS), 1.0, 6.0, ((1, 8), (2, 16)), jnp.float32),
        "warmth_anomaly": scatter_about(streams_of[2], (VERTICAL_TIERS, MERIDIAN_POINTS, PARALLEL_POINTS), 1.0, 6.0, ((1, 8), (2, 16)), jnp.float32),
        "brine_anomaly": scatter_about(streams_of[3], (VERTICAL_TIERS, MERIDIAN_POINTS, PARALLEL_POINTS), 1.0, 6.0, ((1, 8), (2, 16)), jnp.float32),
        "marine_indicator": set_ends((jax.random.randint(streams_of[4], (MERIDIAN_POINTS, PARALLEL_POINTS), 0, 4) < 3).astype(jnp.int32), jax.random.fold_in(streams_of[4], 1), 0, 1),
        "retained_tile_indicator": set_ends((jax.random.randint(streams_of[5], (NBY, NBX), 0, 8) < 7).astype(jnp.int32), jax.random.fold_in(streams_of[5], 1), 0, 1),
        "seabed_thickness": jnp.clip(jnp.exp(math.log(2.5) - 2.3025851 * jax.random.uniform(streams_of[6], (MERIDIAN_POINTS, PARALLEL_POINTS), jnp.float32) ** shard_levels(streams_of[6], (MERIDIAN_POINTS, PARALLEL_POINTS), ((0, 8), (1, 16)), -0.2, 0.2)), 0.25, 2.5),
        "elevation_pivot_entry": jnp.clip(jnp.exp(math.log(1.0) - 2.3025851 * jax.random.uniform(streams_of[7], (MERIDIAN_POINTS, PARALLEL_POINTS), jnp.float32) ** shard_levels(streams_of[7], (MERIDIAN_POINTS, PARALLEL_POINTS), ((0, 8), (1, 16)), -0.2, 0.2)), 0.1, 1.0),
    }


time_step = 0.1
viscosity = 0.2
diffusivity = 0.15
thermal = 0.2
haline = 0.8
source_gain = 8.0


def beside_all(field, parity):
    east_cell = jnp.roll(field, -1, axis=-1)
    west_cell = jnp.roll(field, 1, axis=-1)
    north_cell = jnp.concatenate([field[..., 1:, :], parity * field[..., -1:, ::-1]], axis=-2)
    south_cell = jnp.concatenate([jnp.zeros_like(field[..., :1, :]), field[..., :-1, :]], axis=-2)
    return east_cell, west_cell, north_cell, south_cell


def laplace(field, near):
    return near[0] + near[1] + near[2] + near[3] - 4.0 * field


def reference(zonal_current, meridional_current, warmth_anomaly, brine_anomaly, marine_indicator, retained_tile_indicator, seabed_thickness, elevation_pivot_entry):
    marine_snapshot = marine_indicator.astype(jnp.float32)
    rows_global = jnp.arange(MERIDIAN_POINTS).astype(jnp.float32)
    coriolis = (2.0 * (rows_global + 0.5) / MERIDIAN_POINTS - 1.0)[:, None]

    def march_single_tier(iterate_carry, inputs):
        pressure, zonal_sum, merid_sum = iterate_carry
        zonal = inputs[0] * marine_snapshot
        merid = inputs[1] * marine_snapshot
        enthalpy_content = inputs[2] * marine_snapshot
        salt = inputs[3] * marine_snapshot
        pressure = pressure + (haline * salt - thermal * enthalpy_content)
        near_p = beside_all(pressure, 1.0)
        near_u = beside_all(zonal, -1.0)
        near_v = beside_all(merid, -1.0)
        near_t = beside_all(enthalpy_content, 1.0)
        near_s = beside_all(salt, 1.0)
        zonal_new = marine_snapshot * (zonal + time_step * (coriolis * merid - 0.5 * (near_p[0] - near_p[1]) + viscosity * laplace(zonal, near_u)))
        merid_new = marine_snapshot * (merid + time_step * (-coriolis * zonal - 0.5 * (near_p[2] - near_p[3]) + viscosity * laplace(merid, near_v)))
        outs = []
        for tracer, near_q in ((enthalpy_content, near_t), (salt, near_s)):
            flux = 0.5 * (near_u[0] * near_q[0] - near_u[1] * near_q[1] + near_v[2] * near_q[2] - near_v[3] * near_q[3])
            outs.append(marine_snapshot * (tracer + time_step * (-flux + diffusivity * laplace(tracer, near_q))))
        return (pressure, zonal_sum + zonal_new, merid_sum + merid_new), (zonal_new, merid_new, outs[0], outs[1])

    blank_tier = jnp.zeros((MERIDIAN_POINTS, PARALLEL_POINTS), jnp.float32)
    iterate_carry, tier_sequence = lax.scan(march_single_tier, (blank_tier, blank_tier, blank_tier), (zonal_current, meridional_current, warmth_anomaly, brine_anomaly))
    zonal_mean = iterate_carry[1] / VERTICAL_TIERS
    merid_mean = iterate_carry[2] / VERTICAL_TIERS
    kept = jnp.repeat(jnp.repeat(retained_tile_indicator.astype(jnp.float32), BLK, axis=0), BLK, axis=1)
    open_cells = marine_snapshot * kept
    column = seabed_thickness * open_cells
    near_um = beside_all(zonal_mean, -1.0)
    near_vm = beside_all(merid_mean, -1.0)
    rhs = -source_gain * open_cells * 0.5 * (near_um[0] - near_um[1] + near_vm[2] - near_vm[3])
    near_c = beside_all(column, 1.0)
    weights = [0.5 * (column + near_c[0]), 0.5 * (column + near_c[1]), 0.5 * (column + near_c[2]), 0.5 * (column + near_c[3])]
    diag = elevation_pivot_entry + weights[0] + weights[1] + weights[2] + weights[3]

    def apply(vector):
        near_x = beside_all(vector, 1.0)
        return open_cells * (diag * vector - weights[0] * near_x[0] - weights[1] * near_x[1] - weights[2] * near_x[2] - weights[3] * near_x[3])

    solution = jnp.zeros_like(rhs)
    residual = rhs
    precond = residual / diag
    direction = precond
    product_now = jnp.sum(residual * precond)
    for step in range(ITERS):
        image = apply(direction)
        alpha = product_now / jnp.sum(direction * image)
        solution = solution + alpha * direction
        residual = residual - alpha * image
        precond = residual / diag
        product_next = jnp.sum(residual * precond)
        direction = precond + (product_next / product_now) * direction
        product_now = product_next
    return tier_sequence[0], tier_sequence[1], tier_sequence[2], tier_sequence[3], solution, residual
```

```python
import jax
import jax.numpy as jnp
from jax import lax
from jax.sharding import PartitionSpec as P

BLK = 16
ITERS = 3


time_step = 0.1
viscosity = 0.2
diffusivity = 0.15
thermal = 0.2
haline = 0.8
source_gain = 8.0


def allsum(value):
    for axis in ("lon", "lat"):
        count = lax.axis_size(axis)
        if count & (count - 1):
            value = lax.psum(value, axis)
            continue
        bit = 1
        while bit < count:
            value = value + lax.ppermute(value, axis, [(i, i ^ bit) for i in range(count)])
            bit *= 2
    return value


def halos(cells, parity):
    if not isinstance(cells, (list, tuple)):
        cells = [cells]
    lon_count = lax.axis_size("lon")
    lat_count = lax.axis_size("lat")

    def edge(index):
        return jnp.concatenate([item[index] for item in cells], axis=0)

    first_col = edge((Ellipsis, slice(None), slice(0, 1)))
    last_col = edge((Ellipsis, slice(None), slice(-1, None)))
    first_row = edge((Ellipsis, slice(0, 1), slice(None)))
    last_row = edge((Ellipsis, slice(-1, None), slice(None)))
    east = lax.ppermute(first_col, "lon", [((i + 1) % lon_count, i) for i in range(lon_count)])
    west = lax.ppermute(last_col, "lon", [(i, (i + 1) % lon_count) for i in range(lon_count)])
    north = lax.ppermute(first_row, "lat", [(i + 1, i) for i in range(lat_count - 1)])
    south = lax.ppermute(last_row, "lat", [(i, i + 1) for i in range(lat_count - 1)])
    mirror = lax.ppermute(last_row, "lon", [(i, lon_count - 1 - i) for i in range(lon_count)])
    folded = parity * mirror[..., ::-1]
    north = jnp.where(lax.axis_index("lat") == lat_count - 1, folded, north)
    return east, west, north, south


def around(cells, halo):
    east, west, north, south = halo
    return (
        jnp.concatenate([cells[..., :, 1:], east], axis=-1),
        jnp.concatenate([west, cells[..., :, :-1]], axis=-1),
        jnp.concatenate([cells[..., 1:, :], north], axis=-2),
        jnp.concatenate([south, cells[..., :-1, :]], axis=-2),
    )


def laplace(field, near):
    return near[0] + near[1] + near[2] + near[3] - 4.0 * field


def local(
    zonal_current,
    meridional_current,
    warmth_anomaly,
    brine_anomaly,
    marine_indicator,
    retained_tile_indicator,
    seabed_thickness,
    elevation_pivot_entry,
):
    level_fields, height, breadth = zonal_current.shape
    marine_snapshot = marine_indicator.astype(jnp.float32)
    zonal = zonal_current * marine_snapshot
    merid = meridional_current * marine_snapshot
    enthalpy_content = warmth_anomaly * marine_snapshot
    salt = brine_anomaly * marine_snapshot
    kept = jnp.repeat(
        jnp.repeat(retained_tile_indicator.astype(jnp.float32), BLK, axis=0), BLK, axis=1
    )
    open_cells = marine_snapshot * kept
    column = seabed_thickness * open_cells

    stack = [zonal, merid, enthalpy_content, salt, column[None]]
    parity = jnp.concatenate(
        [
            -jnp.ones((2 * level_fields,), jnp.float32),
            jnp.ones((2 * level_fields + 1,), jnp.float32),
        ]
    )[:, None, None]
    halo_all = halos(stack, parity)

    def part(first, count):
        return tuple(item[first : first + count] for item in halo_all)

    near_u = around(zonal, part(0, level_fields))
    near_v = around(merid, part(level_fields, level_fields))
    halo_t = part(2 * level_fields, level_fields)
    halo_s = part(3 * level_fields, level_fields)
    near_t = around(enthalpy_content, halo_t)
    near_s = around(salt, halo_s)
    halo_c = tuple(item[4 * level_fields] for item in halo_all)
    near_c = around(column, halo_c)

    pressure = jnp.cumsum(haline * salt - thermal * enthalpy_content, axis=0)
    halo_p = tuple(
        jnp.cumsum(haline * halo_s[side] - thermal * halo_t[side], axis=0) for side in range(4)
    )
    near_p = around(pressure, halo_p)

    total_rows = height * lax.axis_size("lat")
    rows_global = (lax.axis_index("lat") * height + jnp.arange(height)).astype(jnp.float32)
    coriolis = (2.0 * (rows_global + 0.5) / total_rows - 1.0)[:, None]
    zonal_next = marine_snapshot * (
        zonal
        + time_step
        * (coriolis * merid - 0.5 * (near_p[0] - near_p[1]) + viscosity * laplace(zonal, near_u))
    )
    merid_next = marine_snapshot * (
        merid
        + time_step
        * (-coriolis * zonal - 0.5 * (near_p[2] - near_p[3]) + viscosity * laplace(merid, near_v))
    )
    tracers = []
    for tracer, near_q in ((enthalpy_content, near_t), (salt, near_s)):
        flux = 0.5 * (
            near_u[0] * near_q[0]
            - near_u[1] * near_q[1]
            + near_v[2] * near_q[2]
            - near_v[3] * near_q[3]
        )
        tracers.append(
            marine_snapshot * (tracer + time_step * (-flux + diffusivity * laplace(tracer, near_q)))
        )
    zonal_mean = jnp.sum(zonal_next, axis=0) / level_fields
    merid_mean = jnp.sum(merid_next, axis=0) / level_fields

    means = jnp.stack([zonal_mean, merid_mean], axis=0)
    halo_m = halos([zonal_mean[None], merid_mean[None]], -jnp.ones((2, 1, 1), jnp.float32))
    near_m = around(means, halo_m)
    rhs = (
        -source_gain
        * open_cells
        * 0.5
        * (near_m[0][0] - near_m[1][0] + near_m[2][1] - near_m[3][1])
    )
    weights = [0.5 * (column + near_c[side]) for side in range(4)]
    diag = elevation_pivot_entry + weights[0] + weights[1] + weights[2] + weights[3]
    unit = jnp.ones((), jnp.float32)

    def apply(direction, halo_d):
        near_x = around(direction, halo_d)
        return open_cells * (
            diag * direction
            - weights[0] * near_x[0]
            - weights[1] * near_x[1]
            - weights[2] * near_x[2]
            - weights[3] * near_x[3]
        )

    solution = jnp.zeros_like(rhs)
    residual = rhs
    precond = residual / diag
    direction = precond
    halo_d = halos(direction, unit)
    image = apply(direction, halo_d)
    pair = allsum(jnp.stack([jnp.sum(residual * precond), jnp.sum(direction * image)]))
    product_now = pair[0]
    curvature = pair[1]
    for step in range(ITERS):
        alpha = product_now / curvature
        solution = solution + alpha * direction
        residual = residual - alpha * image
        if step + 1 < ITERS:
            precond = residual / diag
            halo_z = halos(precond, unit)
            product_next = allsum(jnp.sum(residual * precond))
            beta = product_next / product_now
            direction = precond + beta * direction
            halo_d = tuple(hz + beta * hd for hz, hd in zip(halo_z, halo_d))
            product_now = product_next
            image = apply(direction, halo_d)
            curvature = allsum(jnp.sum(direction * image))
    return (zonal_next, merid_next, tracers[0], tracers[1], solution, residual)


def solution(mesh):
    in_specs = (
        P(None, "lat", "lon"),
        P(None, "lat", "lon"),
        P(None, "lat", "lon"),
        P(None, "lat", "lon"),
        P("lat", "lon"),
        P("lat", "lon"),
        P("lat", "lon"),
        P("lat", "lon"),
    )
    out_specs = (
        P(None, "lat", "lon"),
        P(None, "lat", "lon"),
        P(None, "lat", "lon"),
        P(None, "lat", "lon"),
        P("lat", "lon"),
        P("lat", "lon"),
    )
    return jax.shard_map(local, mesh=mesh, in_specs=in_specs, out_specs=out_specs, check_vma=False)
```

```python
import jax
import jax.numpy as jnp
from jax import lax
from jax.sharding import PartitionSpec as P

BLK = 16
ITERS = 3


time_step = 0.1
viscosity = 0.2
diffusivity = 0.15
thermal = 0.2
haline = 0.8
source_gain = 8.0


def allsum(value):
    count = lax.axis_size("lon") * lax.axis_size("lat")
    spread = jnp.broadcast_to(value, (count,) + jnp.shape(value))
    gathered = lax.all_to_all(spread, ("lon", "lat"), 0, 0, tiled=True)
    return jnp.sum(gathered, axis=0)


def halos(cells, parity):
    if not isinstance(cells, (list, tuple)):
        cells = [cells]
    lon_count = lax.axis_size("lon")
    lat_count = lax.axis_size("lat")

    def edge(index):
        return jnp.concatenate([item[index] for item in cells], axis=0)

    first_col = edge((Ellipsis, slice(None), slice(0, 1)))
    last_col = edge((Ellipsis, slice(None), slice(-1, None)))
    first_row = edge((Ellipsis, slice(0, 1), slice(None)))
    last_row = edge((Ellipsis, slice(-1, None), slice(None)))
    east = lax.ppermute(first_col, "lon", [((i + 1) % lon_count, i) for i in range(lon_count)])
    west = lax.ppermute(last_col, "lon", [(i, (i + 1) % lon_count) for i in range(lon_count)])
    north = lax.ppermute(first_row, "lat", [(i + 1, i) for i in range(lat_count - 1)])
    south = lax.ppermute(last_row, "lat", [(i, i + 1) for i in range(lat_count - 1)])
    mirror = lax.ppermute(last_row, "lon", [(i, lon_count - 1 - i) for i in range(lon_count)])
    folded = parity * mirror[..., ::-1]
    north = jnp.where(lax.axis_index("lat") == lat_count - 1, folded, north)
    return east, west, north, south


def around(cells, halo):
    east, west, north, south = halo
    return (
        jnp.concatenate([cells[..., :, 1:], east], axis=-1),
        jnp.concatenate([west, cells[..., :, :-1]], axis=-1),
        jnp.concatenate([cells[..., 1:, :], north], axis=-2),
        jnp.concatenate([south, cells[..., :-1, :]], axis=-2),
    )


def laplace(field, near):
    return near[0] + near[1] + near[2] + near[3] - 4.0 * field


def local(
    zonal_current,
    meridional_current,
    warmth_anomaly,
    brine_anomaly,
    marine_indicator,
    retained_tile_indicator,
    seabed_thickness,
    elevation_pivot_entry,
):
    level_fields, height, breadth = zonal_current.shape
    marine_snapshot = marine_indicator.astype(jnp.float32)
    zonal = zonal_current * marine_snapshot
    merid = meridional_current * marine_snapshot
    enthalpy_content = warmth_anomaly * marine_snapshot
    salt = brine_anomaly * marine_snapshot
    kept = jnp.repeat(
        jnp.repeat(retained_tile_indicator.astype(jnp.float32), BLK, axis=0), BLK, axis=1
    )
    open_cells = marine_snapshot * kept
    column = seabed_thickness * open_cells

    stack = [zonal, merid, enthalpy_content, salt, column[None]]
    parity = jnp.concatenate(
        [
            -jnp.ones((2 * level_fields,), jnp.float32),
            jnp.ones((2 * level_fields + 1,), jnp.float32),
        ]
    )[:, None, None]
    halo_all = halos(stack, parity)

    def part(first, count):
        return tuple(item[first : first + count] for item in halo_all)

    near_u = around(zonal, part(0, level_fields))
    near_v = around(merid, part(level_fields, level_fields))
    halo_t = part(2 * level_fields, level_fields)
    halo_s = part(3 * level_fields, level_fields)
    near_t = around(enthalpy_content, halo_t)
    near_s = around(salt, halo_s)
    halo_c = tuple(item[4 * level_fields] for item in halo_all)
    near_c = around(column, halo_c)

    pressure = jnp.cumsum(haline * salt - thermal * enthalpy_content, axis=0)
    halo_p = tuple(
        jnp.cumsum(haline * halo_s[side] - thermal * halo_t[side], axis=0) for side in range(4)
    )
    near_p = around(pressure, halo_p)

    total_rows = height * lax.axis_size("lat")
    rows_global = (lax.axis_index("lat") * height + jnp.arange(height)).astype(jnp.float32)
    coriolis = (2.0 * (rows_global + 0.5) / total_rows - 1.0)[:, None]
    zonal_next = marine_snapshot * (
        zonal
        + time_step
        * (coriolis * merid - 0.5 * (near_p[0] - near_p[1]) + viscosity * laplace(zonal, near_u))
    )
    merid_next = marine_snapshot * (
        merid
        + time_step
        * (-coriolis * zonal - 0.5 * (near_p[2] - near_p[3]) + viscosity * laplace(merid, near_v))
    )
    tracers = []
    for tracer, near_q in ((enthalpy_content, near_t), (salt, near_s)):
        flux = 0.5 * (
            near_u[0] * near_q[0]
            - near_u[1] * near_q[1]
            + near_v[2] * near_q[2]
            - near_v[3] * near_q[3]
        )
        tracers.append(
            marine_snapshot * (tracer + time_step * (-flux + diffusivity * laplace(tracer, near_q)))
        )
    zonal_mean = jnp.sum(zonal_next, axis=0) / level_fields
    merid_mean = jnp.sum(merid_next, axis=0) / level_fields

    means = jnp.stack([zonal_mean, merid_mean], axis=0)
    halo_m = halos([zonal_mean[None], merid_mean[None]], -jnp.ones((2, 1, 1), jnp.float32))
    near_m = around(means, halo_m)
    rhs = (
        -source_gain
        * open_cells
        * 0.5
        * (near_m[0][0] - near_m[1][0] + near_m[2][1] - near_m[3][1])
    )
    weights = [0.5 * (column + near_c[side]) for side in range(4)]
    diag = elevation_pivot_entry + weights[0] + weights[1] + weights[2] + weights[3]
    unit = jnp.ones((), jnp.float32)

    def apply(direction, halo_d):
        near_x = around(direction, halo_d)
        return open_cells * (
            diag * direction
            - weights[0] * near_x[0]
            - weights[1] * near_x[1]
            - weights[2] * near_x[2]
            - weights[3] * near_x[3]
        )

    solution = jnp.zeros_like(rhs)
    residual = rhs
    precond = residual / diag
    direction = precond
    halo_d = halos(direction, unit)
    image = apply(direction, halo_d)
    pair = allsum(jnp.stack([jnp.sum(residual * precond), jnp.sum(direction * image)]))
    product_now = pair[0]
    curvature = pair[1]
    for step in range(ITERS):
        alpha = product_now / curvature
        solution = solution + alpha * direction
        residual = residual - alpha * image
        if step + 1 < ITERS:
            precond = residual / diag
            halo_z = halos(precond, unit)
            product_next = allsum(jnp.sum(residual * precond))
            beta = product_next / product_now
            direction = precond + beta * direction
            halo_d = tuple(hz + beta * hd for hz, hd in zip(halo_z, halo_d))
            product_now = product_next
            image = apply(direction, halo_d)
            curvature = allsum(jnp.sum(direction * image))
    return (zonal_next, merid_next, tracers[0], tracers[1], solution, residual)


def solution(mesh):
    in_specs = (
        P(None, "lat", "lon"),
        P(None, "lat", "lon"),
        P(None, "lat", "lon"),
        P(None, "lat", "lon"),
        P("lat", "lon"),
        P("lat", "lon"),
        P("lat", "lon"),
        P("lat", "lon"),
    )
    out_specs = (
        P(None, "lat", "lon"),
        P(None, "lat", "lon"),
        P(None, "lat", "lon"),
        P(None, "lat", "lon"),
        P("lat", "lon"),
        P("lat", "lon"),
    )
    return jax.shard_map(local, mesh=mesh, in_specs=in_specs, out_specs=out_specs, check_vma=False)
```

```python
import jax
import jax.numpy as jnp
from jax import lax
from jax.sharding import PartitionSpec as P

BLK = 16
ITERS = 3


time_step = 0.1
viscosity = 0.2
diffusivity = 0.15
thermal = 0.2
haline = 0.8
source_gain = 8.0


def allsum(value):
    count = lax.axis_size("lon") * lax.axis_size("lat")
    spread = jnp.broadcast_to(value, (count,) + jnp.shape(value))
    gathered = lax.all_to_all(spread, ("lon", "lat"), 0, 0, tiled=True)
    return jnp.sum(gathered, axis=0)


def halos(cells, parity):
    if not isinstance(cells, (list, tuple)):
        cells = [cells]
    lon_count = lax.axis_size("lon")
    lat_count = lax.axis_size("lat")

    def edge(index):
        return jnp.concatenate([item[index] for item in cells], axis=0)

    first_col = edge((Ellipsis, slice(None), slice(0, 1)))
    last_col = edge((Ellipsis, slice(None), slice(-1, None)))
    first_row = edge((Ellipsis, slice(0, 1), slice(None)))
    last_row = edge((Ellipsis, slice(-1, None), slice(None)))
    east = lax.ppermute(first_col, "lon", [((i + 1) % lon_count, i) for i in range(lon_count)])
    west = lax.ppermute(last_col, "lon", [(i, (i + 1) % lon_count) for i in range(lon_count)])
    north = lax.ppermute(first_row, "lat", [(i + 1, i) for i in range(lat_count - 1)])
    south = lax.ppermute(last_row, "lat", [(i, i + 1) for i in range(lat_count - 1)])
    mirror = lax.ppermute(last_row, "lon", [(i, lon_count - 1 - i) for i in range(lon_count)])
    folded = parity * mirror[..., ::-1]
    north = jnp.where(lax.axis_index("lat") == lat_count - 1, folded, north)
    return east, west, north, south


def around(cells, halo):
    east, west, north, south = halo
    return (
        jnp.concatenate([cells[..., :, 1:], east], axis=-1),
        jnp.concatenate([west, cells[..., :, :-1]], axis=-1),
        jnp.concatenate([cells[..., 1:, :], north], axis=-2),
        jnp.concatenate([south, cells[..., :-1, :]], axis=-2),
    )


def laplace(field, near):
    return near[0] + near[1] + near[2] + near[3] - 4.0 * field


def local(
    zonal_current,
    meridional_current,
    warmth_anomaly,
    brine_anomaly,
    marine_indicator,
    retained_tile_indicator,
    seabed_thickness,
    elevation_pivot_entry,
):
    level_fields, height, breadth = zonal_current.shape
    marine_snapshot = marine_indicator.astype(jnp.float32)
    zonal = zonal_current * marine_snapshot
    merid = meridional_current * marine_snapshot
    enthalpy_content = warmth_anomaly * marine_snapshot
    salt = brine_anomaly * marine_snapshot
    kept = jnp.repeat(
        jnp.repeat(retained_tile_indicator.astype(jnp.float32), BLK, axis=0), BLK, axis=1
    )
    open_cells = marine_snapshot * kept
    column = seabed_thickness * open_cells

    stack = [zonal, merid, enthalpy_content, salt, column[None]]
    parity = jnp.concatenate(
        [
            -jnp.ones((2 * level_fields,), jnp.float32),
            jnp.ones((2 * level_fields + 1,), jnp.float32),
        ]
    )[:, None, None]
    halo_all = halos(stack, parity)

    def part(first, count):
        return tuple(item[first : first + count] for item in halo_all)

    near_u = around(zonal, part(0, level_fields))
    near_v = around(merid, part(level_fields, level_fields))
    halo_t = part(2 * level_fields, level_fields)
    halo_s = part(3 * level_fields, level_fields)
    near_t = around(enthalpy_content, halo_t)
    near_s = around(salt, halo_s)
    halo_c = tuple(item[4 * level_fields] for item in halo_all)
    near_c = around(column, halo_c)

    pressure = jnp.cumsum(haline * salt - thermal * enthalpy_content, axis=0)
    halo_p = tuple(
        jnp.cumsum(haline * halo_s[side] - thermal * halo_t[side], axis=0) for side in range(4)
    )
    near_p = around(pressure, halo_p)

    total_rows = height * lax.axis_size("lat")
    rows_global = (lax.axis_index("lat") * height + jnp.arange(height)).astype(jnp.float32)
    coriolis = (2.0 * (rows_global + 0.5) / total_rows - 1.0)[:, None]
    zonal_next = marine_snapshot * (
        zonal
        + time_step
        * (coriolis * merid - 0.5 * (near_p[0] - near_p[1]) + viscosity * laplace(zonal, near_u))
    )
    merid_next = marine_snapshot * (
        merid
        + time_step
        * (-coriolis * zonal - 0.5 * (near_p[2] - near_p[3]) + viscosity * laplace(merid, near_v))
    )
    tracers = []
    for tracer, near_q in ((enthalpy_content, near_t), (salt, near_s)):
        flux = 0.5 * (
            near_u[0] * near_q[0]
            - near_u[1] * near_q[1]
            + near_v[2] * near_q[2]
            - near_v[3] * near_q[3]
        )
        tracers.append(
            marine_snapshot * (tracer + time_step * (-flux + diffusivity * laplace(tracer, near_q)))
        )
    zonal_mean = jnp.sum(zonal_next, axis=0) / level_fields
    merid_mean = jnp.sum(merid_next, axis=0) / level_fields

    means = jnp.stack([zonal_mean, merid_mean], axis=0)
    halo_m = halos([zonal_mean[None], merid_mean[None]], -jnp.ones((2, 1, 1), jnp.float32))
    near_m = around(means, halo_m)
    rhs = (
        -source_gain
        * open_cells
        * 0.5
        * (near_m[0][0] - near_m[1][0] + near_m[2][1] - near_m[3][1])
    )
    weights = [0.5 * (column + near_c[side]) for side in range(4)]
    diag = elevation_pivot_entry + weights[0] + weights[1] + weights[2] + weights[3]
    unit = jnp.ones((), jnp.float32)

    def apply(direction, halo_d):
        near_x = around(direction, halo_d)
        return open_cells * (
            diag * direction
            - weights[0] * near_x[0]
            - weights[1] * near_x[1]
            - weights[2] * near_x[2]
            - weights[3] * near_x[3]
        )

    solution = jnp.zeros_like(rhs)
    residual = rhs
    precond = residual / diag
    direction = precond
    image = apply(direction, halos(direction, unit))
    pair = allsum(jnp.stack([jnp.sum(residual * precond), jnp.sum(direction * image)]))
    product_now = pair[0]
    curvature = pair[1]
    for step in range(ITERS):
        alpha = product_now / curvature
        solution = solution + alpha * direction
        residual = residual - alpha * image
        if step + 1 < ITERS:
            precond = residual / diag
            image_z = apply(precond, halos(precond, unit))
            sums = allsum(
                jnp.stack(
                    [
                        jnp.sum(residual * precond),
                        jnp.sum(precond * image_z),
                        jnp.sum(precond * image),
                        jnp.sum(direction * image_z),
                    ]
                )
            )
            product_next = sums[0]
            beta = product_next / product_now
            curvature = sums[1] + beta * (sums[2] + sums[3]) + beta * beta * curvature
            direction = precond + beta * direction
            image = image_z + beta * image
            product_now = product_next
    return (zonal_next, merid_next, tracers[0], tracers[1], solution, residual)


def solution(mesh):
    in_specs = (
        P(None, "lat", "lon"),
        P(None, "lat", "lon"),
        P(None, "lat", "lon"),
        P(None, "lat", "lon"),
        P("lat", "lon"),
        P("lat", "lon"),
        P("lat", "lon"),
        P("lat", "lon"),
    )
    out_specs = (
        P(None, "lat", "lon"),
        P(None, "lat", "lon"),
        P(None, "lat", "lon"),
        P(None, "lat", "lon"),
        P("lat", "lon"),
        P("lat", "lon"),
    )
    return jax.shard_map(local, mesh=mesh, in_specs=in_specs, out_specs=out_specs, check_vma=False)
```

```python
import jax
import jax.numpy as jnp
from jax import lax
from jax.sharding import PartitionSpec as P

BLK = 16
ITERS = 3


time_step = 0.1
viscosity = 0.2
diffusivity = 0.15
thermal = 0.2
haline = 0.8
source_gain = 8.0


def allsum(value):
    count = lax.axis_size("lon") * lax.axis_size("lat")
    spread = jnp.broadcast_to(value, (count,) + jnp.shape(value))
    gathered = lax.all_to_all(spread, ("lon", "lat"), 0, 0, tiled=True)
    return jnp.sum(gathered, axis=0)


def halos(cells, parity):
    if not isinstance(cells, (list, tuple)):
        cells = [cells]
    lon_count = lax.axis_size("lon")
    lat_count = lax.axis_size("lat")

    def edge(index):
        return jnp.concatenate([item[index] for item in cells], axis=0)

    first_col = edge((Ellipsis, slice(None), 0))
    last_col = edge((Ellipsis, slice(None), -1))
    first_row = edge((Ellipsis, slice(0, 1), slice(None)))
    last_row = edge((Ellipsis, slice(-1, None), slice(None)))
    east = lax.ppermute(first_col, "lon", [((i + 1) % lon_count, i) for i in range(lon_count)])
    west = lax.ppermute(last_col, "lon", [(i, (i + 1) % lon_count) for i in range(lon_count)])
    north = lax.ppermute(first_row, "lat", [(i + 1, i) for i in range(lat_count - 1)])
    south = lax.ppermute(last_row, "lat", [(i, i + 1) for i in range(lat_count - 1)])
    top = lat_count - 1
    mirror = lax.ppermute(
        last_row,
        ("lon", "lat"),
        [(i * lat_count + top, (lon_count - 1 - i) * lat_count + top) for i in range(lon_count)],
    )
    folded = parity * mirror[..., ::-1]
    north = jnp.where(lax.axis_index("lat") == top, folded, north)
    return east, west, north, south


def around(cells, halo):
    east, west, north, south = halo
    return (
        jnp.concatenate([cells[..., :, 1:], east[..., None]], axis=-1),
        jnp.concatenate([west[..., None], cells[..., :, :-1]], axis=-1),
        jnp.concatenate([cells[..., 1:, :], north], axis=-2),
        jnp.concatenate([south, cells[..., :-1, :]], axis=-2),
    )


def laplace(field, near):
    return near[0] + near[1] + near[2] + near[3] - 4.0 * field


def local(
    zonal_current,
    meridional_current,
    warmth_anomaly,
    brine_anomaly,
    marine_indicator,
    retained_tile_indicator,
    seabed_thickness,
    elevation_pivot_entry,
):
    level_fields, height, breadth = zonal_current.shape
    marine_snapshot = marine_indicator.astype(jnp.float32)
    zonal = zonal_current * marine_snapshot
    merid = meridional_current * marine_snapshot
    enthalpy_content = warmth_anomaly * marine_snapshot
    salt = brine_anomaly * marine_snapshot
    kept = jnp.repeat(
        jnp.repeat(retained_tile_indicator.astype(jnp.float32), BLK, axis=0), BLK, axis=1
    )
    open_cells = marine_snapshot * kept
    column = seabed_thickness * open_cells

    stack = [zonal, merid, enthalpy_content, salt, column[None]]
    parity = jnp.concatenate(
        [
            -jnp.ones((2 * level_fields,), jnp.float32),
            jnp.ones((2 * level_fields + 1,), jnp.float32),
        ]
    )[:, None, None]
    halo_all = halos(stack, parity)

    def part(first, count):
        return tuple(item[first : first + count] for item in halo_all)

    near_u = around(zonal, part(0, level_fields))
    near_v = around(merid, part(level_fields, level_fields))
    halo_t = part(2 * level_fields, level_fields)
    halo_s = part(3 * level_fields, level_fields)
    near_t = around(enthalpy_content, halo_t)
    near_s = around(salt, halo_s)
    halo_c = tuple(item[4 * level_fields] for item in halo_all)
    near_c = around(column, halo_c)

    pressure = jnp.cumsum(haline * salt - thermal * enthalpy_content, axis=0)
    halo_p = tuple(
        jnp.cumsum(haline * halo_s[side] - thermal * halo_t[side], axis=0) for side in range(4)
    )
    near_p = around(pressure, halo_p)

    total_rows = height * lax.axis_size("lat")
    rows_global = (lax.axis_index("lat") * height + jnp.arange(height)).astype(jnp.float32)
    coriolis = (2.0 * (rows_global + 0.5) / total_rows - 1.0)[:, None]
    zonal_next = marine_snapshot * (
        zonal
        + time_step
        * (coriolis * merid - 0.5 * (near_p[0] - near_p[1]) + viscosity * laplace(zonal, near_u))
    )
    merid_next = marine_snapshot * (
        merid
        + time_step
        * (-coriolis * zonal - 0.5 * (near_p[2] - near_p[3]) + viscosity * laplace(merid, near_v))
    )
    tracers = []
    for tracer, near_q in ((enthalpy_content, near_t), (salt, near_s)):
        flux = 0.5 * (
            near_u[0] * near_q[0]
            - near_u[1] * near_q[1]
            + near_v[2] * near_q[2]
            - near_v[3] * near_q[3]
        )
        tracers.append(
            marine_snapshot * (tracer + time_step * (-flux + diffusivity * laplace(tracer, near_q)))
        )
    zonal_mean = jnp.sum(zonal_next, axis=0) / level_fields
    merid_mean = jnp.sum(merid_next, axis=0) / level_fields

    means = jnp.stack([zonal_mean, merid_mean], axis=0)
    halo_m = halos([zonal_mean[None], merid_mean[None]], -jnp.ones((2, 1, 1), jnp.float32))
    near_m = around(means, halo_m)
    rhs = (
        -source_gain
        * open_cells
        * 0.5
        * (near_m[0][0] - near_m[1][0] + near_m[2][1] - near_m[3][1])
    )
    weights = [0.5 * (column + near_c[side]) for side in range(4)]
    diag = elevation_pivot_entry + weights[0] + weights[1] + weights[2] + weights[3]
    unit = jnp.ones((), jnp.float32)

    def apply(direction, halo_d):
        near_x = around(direction, halo_d)
        return open_cells * (
            diag * direction
            - weights[0] * near_x[0]
            - weights[1] * near_x[1]
            - weights[2] * near_x[2]
            - weights[3] * near_x[3]
        )

    solution = jnp.zeros_like(rhs)
    residual = rhs
    precond = residual / diag
    direction = precond
    image = apply(direction, halos(direction, unit))
    pair = allsum(jnp.stack([jnp.sum(residual * precond), jnp.sum(direction * image)]))
    product_now = pair[0]
    curvature = pair[1]
    for step in range(ITERS):
        alpha = product_now / curvature
        solution = solution + alpha * direction
        residual = residual - alpha * image
        if step + 1 < ITERS:
            precond = residual / diag
            image_z = apply(precond, halos(precond, unit))
            sums = allsum(
                jnp.stack(
                    [
                        jnp.sum(residual * precond),
                        jnp.sum(precond * image_z),
                        jnp.sum(precond * image),
                        jnp.sum(direction * image_z),
                    ]
                )
            )
            product_next = sums[0]
            beta = product_next / product_now
            curvature = sums[1] + beta * (sums[2] + sums[3]) + beta * beta * curvature
            direction = precond + beta * direction
            image = image_z + beta * image
            product_now = product_next
    return (zonal_next, merid_next, tracers[0], tracers[1], solution, residual)


def solution(mesh):
    in_specs = (
        P(None, "lat", "lon"),
        P(None, "lat", "lon"),
        P(None, "lat", "lon"),
        P(None, "lat", "lon"),
        P("lat", "lon"),
        P("lat", "lon"),
        P("lat", "lon"),
        P("lat", "lon"),
    )
    out_specs = (
        P(None, "lat", "lon"),
        P(None, "lat", "lon"),
        P(None, "lat", "lon"),
        P(None, "lat", "lon"),
        P("lat", "lon"),
        P("lat", "lon"),
    )
    return jax.shard_map(local, mesh=mesh, in_specs=in_specs, out_specs=out_specs, check_vma=False)
```

```python
import jax
import jax.numpy as jnp
from jax import lax
from jax.sharding import PartitionSpec as P

BLK = 16
ITERS = 3


time_step = 0.1
viscosity = 0.2
diffusivity = 0.15
thermal = 0.2
haline = 0.8
source_gain = 8.0


def allsum(value):
    count = lax.axis_size("lon") * lax.axis_size("lat")
    spread = jnp.broadcast_to(value, (count,) + jnp.shape(value))
    gathered = lax.all_to_all(spread, ("lon", "lat"), 0, 0, tiled=True)
    return jnp.sum(gathered, axis=0)


def halos(cells, parity):
    if not isinstance(cells, (list, tuple)):
        cells = [cells]
    lon_count = lax.axis_size("lon")
    lat_count = lax.axis_size("lat")

    def edge(index):
        return jnp.concatenate([item[index] for item in cells], axis=0)

    first_col = edge((Ellipsis, slice(None), 0))
    last_col = edge((Ellipsis, slice(None), -1))
    first_row = edge((Ellipsis, slice(0, 1), slice(None)))
    last_row = edge((Ellipsis, slice(-1, None), slice(None)))
    east = lax.ppermute(first_col, "lon", [((i + 1) % lon_count, i) for i in range(lon_count)])
    west = lax.ppermute(last_col, "lon", [(i, (i + 1) % lon_count) for i in range(lon_count)])
    north = lax.ppermute(first_row, "lat", [(i + 1, i) for i in range(lat_count - 1)])
    south = lax.ppermute(last_row, "lat", [(i, i + 1) for i in range(lat_count - 1)])
    top = lat_count - 1
    mirror = lax.ppermute(
        last_row,
        ("lon", "lat"),
        [(i * lat_count + top, (lon_count - 1 - i) * lat_count + top) for i in range(lon_count)],
    )
    folded = parity * mirror[..., ::-1]
    north = jnp.where(lax.axis_index("lat") == top, folded, north)
    return east, west, north, south


def around(cells, halo):
    east, west, north, south = halo
    return (
        jnp.concatenate([cells[..., :, 1:], east[..., None]], axis=-1),
        jnp.concatenate([west[..., None], cells[..., :, :-1]], axis=-1),
        jnp.concatenate([cells[..., 1:, :], north], axis=-2),
        jnp.concatenate([south, cells[..., :-1, :]], axis=-2),
    )


def laplace(field, near):
    return near[0] + near[1] + near[2] + near[3] - 4.0 * field


def local(
    zonal_current,
    meridional_current,
    warmth_anomaly,
    brine_anomaly,
    marine_indicator,
    retained_tile_indicator,
    seabed_thickness,
    elevation_pivot_entry,
):
    level_fields, height, breadth = zonal_current.shape
    marine_snapshot = marine_indicator.astype(jnp.float32)
    zonal = zonal_current * marine_snapshot
    merid = meridional_current * marine_snapshot
    enthalpy_content = warmth_anomaly * marine_snapshot
    salt = brine_anomaly * marine_snapshot
    kept = jnp.repeat(
        jnp.repeat(retained_tile_indicator.astype(jnp.float32), BLK, axis=0), BLK, axis=1
    )
    open_cells = marine_snapshot * kept
    column = seabed_thickness * open_cells

    stack = [zonal, merid, enthalpy_content, salt, column[None]]
    parity = jnp.concatenate(
        [
            -jnp.ones((2 * level_fields,), jnp.float32),
            jnp.ones((2 * level_fields + 1,), jnp.float32),
        ]
    )[:, None, None]
    halo_all = halos(stack, parity)

    def part(first, count):
        return tuple(item[first : first + count] for item in halo_all)

    near_u = around(zonal, part(0, level_fields))
    near_v = around(merid, part(level_fields, level_fields))
    halo_t = part(2 * level_fields, level_fields)
    halo_s = part(3 * level_fields, level_fields)
    near_t = around(enthalpy_content, halo_t)
    near_s = around(salt, halo_s)
    halo_c = tuple(item[4 * level_fields] for item in halo_all)
    near_c = around(column, halo_c)

    pressure = jnp.cumsum(haline * salt - thermal * enthalpy_content, axis=0)
    halo_p = tuple(
        jnp.cumsum(haline * halo_s[side] - thermal * halo_t[side], axis=0) for side in range(4)
    )
    near_p = around(pressure, halo_p)

    total_rows = height * lax.axis_size("lat")
    rows_global = (lax.axis_index("lat") * height + jnp.arange(height)).astype(jnp.float32)
    coriolis = (2.0 * (rows_global + 0.5) / total_rows - 1.0)[:, None]
    zonal_next = marine_snapshot * (
        zonal
        + time_step
        * (coriolis * merid - 0.5 * (near_p[0] - near_p[1]) + viscosity * laplace(zonal, near_u))
    )
    merid_next = marine_snapshot * (
        merid
        + time_step
        * (-coriolis * zonal - 0.5 * (near_p[2] - near_p[3]) + viscosity * laplace(merid, near_v))
    )
    tracers = []
    for tracer, near_q in ((enthalpy_content, near_t), (salt, near_s)):
        flux = 0.5 * (
            near_u[0] * near_q[0]
            - near_u[1] * near_q[1]
            + near_v[2] * near_q[2]
            - near_v[3] * near_q[3]
        )
        tracers.append(
            marine_snapshot * (tracer + time_step * (-flux + diffusivity * laplace(tracer, near_q)))
        )
    zonal_mean = jnp.sum(zonal_next, axis=0) / level_fields
    merid_mean = jnp.sum(merid_next, axis=0) / level_fields

    means = jnp.stack([zonal_mean, merid_mean], axis=0)
    halo_m = halos([zonal_mean[None], merid_mean[None]], -jnp.ones((2, 1, 1), jnp.float32))
    near_m = around(means, halo_m)
    rhs = (
        -source_gain
        * open_cells
        * 0.5
        * (near_m[0][0] - near_m[1][0] + near_m[2][1] - near_m[3][1])
    )
    weights = [0.5 * (column + near_c[side]) for side in range(4)]
    diag = elevation_pivot_entry + weights[0] + weights[1] + weights[2] + weights[3]
    unit = jnp.ones((), jnp.float32)

    def apply(direction, halo_d):
        near_x = around(direction, halo_d)
        return open_cells * (
            diag * direction
            - weights[0] * near_x[0]
            - weights[1] * near_x[1]
            - weights[2] * near_x[2]
            - weights[3] * near_x[3]
        )

    solution = jnp.zeros_like(rhs)
    residual = rhs
    precond = residual / diag
    direction = precond
    image = apply(direction, halos(direction, unit))
    pair = allsum(jnp.sum(jnp.stack([residual * precond, direction * image]), axis=(1, 2)))
    product_now = pair[0]
    curvature = pair[1]
    for step in range(ITERS):
        alpha = product_now / curvature
        solution = solution + alpha * direction
        residual = residual - alpha * image
        if step + 1 < ITERS:
            precond = residual / diag
            image_z = apply(precond, halos(precond, unit))
            sums = allsum(
                jnp.sum(
                    jnp.stack(
                        [residual * precond, precond * image_z, precond * image, direction * image_z]
                    ),
                    axis=(1, 2),
                )
            )
            product_next = sums[0]
            beta = product_next / product_now
            curvature = sums[1] + beta * (sums[2] + sums[3]) + beta * beta * curvature
            direction = precond + beta * direction
            image = image_z + beta * image
            product_now = product_next
    return (zonal_next, merid_next, tracers[0], tracers[1], solution, residual)


def solution(mesh):
    in_specs = (
        P(None, "lat", "lon"),
        P(None, "lat", "lon"),
        P(None, "lat", "lon"),
        P(None, "lat", "lon"),
        P("lat", "lon"),
        P("lat", "lon"),
        P("lat", "lon"),
        P("lat", "lon"),
    )
    out_specs = (
        P(None, "lat", "lon"),
        P(None, "lat", "lon"),
        P(None, "lat", "lon"),
        P(None, "lat", "lon"),
        P("lat", "lon"),
        P("lat", "lon"),
    )
    return jax.shard_map(local, mesh=mesh, in_specs=in_specs, out_specs=out_specs, check_vma=False)
```

```python
import jax
import jax.numpy as jnp
from jax import lax
from jax.sharding import PartitionSpec as P
from jax.experimental import pallas as pl
from jax.experimental.pallas import tpu as pltpu

INTERPRET = False

BLK = 16
ITERS = 3


time_step = 0.1
viscosity = 0.2
diffusivity = 0.15
thermal = 0.2
haline = 0.8
source_gain = 8.0


def allsum(value):
    count = lax.axis_size("lon") * lax.axis_size("lat")
    spread = jnp.broadcast_to(value, (count,) + jnp.shape(value))
    gathered = lax.all_to_all(spread, ("lon", "lat"), 0, 0, tiled=True)
    return jnp.sum(gathered, axis=0)


def exchange(first_col, last_col, first_row, last_row, parity):
    lon_count = lax.axis_size("lon")
    lat_count = lax.axis_size("lat")
    east = lax.ppermute(first_col, "lon", [((i + 1) % lon_count, i) for i in range(lon_count)])
    west = lax.ppermute(last_col, "lon", [(i, (i + 1) % lon_count) for i in range(lon_count)])
    north = lax.ppermute(first_row, "lat", [(i + 1, i) for i in range(lat_count - 1)])
    south = lax.ppermute(last_row, "lat", [(i, i + 1) for i in range(lat_count - 1)])
    top = lat_count - 1
    mirror = lax.ppermute(
        last_row,
        ("lon", "lat"),
        [(i * lat_count + top, (lon_count - 1 - i) * lat_count + top) for i in range(lon_count)],
    )
    folded = parity * mirror[..., ::-1]
    north = jnp.where(lax.axis_index("lat") == top, folded, north)
    return east, west, north, south


def halos(cells, parity):
    return exchange(cells[..., :, 0], cells[..., :, -1], cells[..., 0, :], cells[..., -1, :], parity)


def around(cells, halo):
    east, west, north, south = halo
    return (
        jnp.concatenate([cells[..., :, 1:], east[..., None]], axis=-1),
        jnp.concatenate([west[..., None], cells[..., :, :-1]], axis=-1),
        jnp.concatenate([cells[..., 1:, :], north[..., None, :]], axis=-2),
        jnp.concatenate([south[..., None, :], cells[..., :-1, :]], axis=-2),
    )


def column_kernel(
    u_ref, v_ref, t_ref, s_ref, m_ref, f_ref, he_ref, hw_ref, hn_ref, hs_ref,
    un_ref, vn_ref, tn_ref, sn_ref, um_ref, vm_ref,
):
    levels, height, breadth = u_ref.shape
    marine = m_ref[...]
    coriolis = f_ref[...]
    row = lax.broadcasted_iota(jnp.int32, (height, breadth), 0)
    col = lax.broadcasted_iota(jnp.int32, (height, breadth), 1)
    last_row = row == height - 1
    first_row = row == 0
    last_col = col == breadth - 1
    first_col = col == 0

    def near(q, e, w, n, s):
        return (
            jnp.where(last_col, e, pltpu.roll(q, breadth - 1, 1)),
            jnp.where(first_col, w, pltpu.roll(q, 1, 1)),
            jnp.where(last_row, n, pltpu.roll(q, height - 1, 0)),
            jnp.where(first_row, s, pltpu.roll(q, 1, 0)),
        )

    def side(index):
        return he_ref[index], hw_ref[index], hn_ref[index], hs_ref[index]

    def body(level, carry):
        pressure, pe, pw, pn, ps, zonal_sum, merid_sum = carry
        zonal = u_ref[level] * marine
        merid = v_ref[level] * marine
        enthalpy_content = t_ref[level] * marine
        salt = s_ref[level] * marine
        halo_u = side(level)
        halo_v = side(levels + level)
        halo_t = side(2 * levels + level)
        halo_s = side(3 * levels + level)
        pressure = pressure + (haline * salt - thermal * enthalpy_content)
        pe = pe + (haline * halo_s[0] - thermal * halo_t[0])
        pw = pw + (haline * halo_s[1] - thermal * halo_t[1])
        pn = pn + (haline * halo_s[2] - thermal * halo_t[2])
        ps = ps + (haline * halo_s[3] - thermal * halo_t[3])
        near_p = near(pressure, pe, pw, pn, ps)
        near_u = near(zonal, *halo_u)
        near_v = near(merid, *halo_v)
        near_t = near(enthalpy_content, *halo_t)
        near_s = near(salt, *halo_s)
        zonal_new = marine * (
            zonal
            + time_step
            * (coriolis * merid - 0.5 * (near_p[0] - near_p[1]) + viscosity * laplace(zonal, near_u))
        )
        merid_new = marine * (
            merid
            + time_step
            * (-coriolis * zonal - 0.5 * (near_p[2] - near_p[3]) + viscosity * laplace(merid, near_v))
        )
        un_ref[level] = zonal_new
        vn_ref[level] = merid_new
        for tracer, near_q, out_ref in ((enthalpy_content, near_t, tn_ref), (salt, near_s, sn_ref)):
            flux = 0.5 * (
                near_u[0] * near_q[0]
                - near_u[1] * near_q[1]
                + near_v[2] * near_q[2]
                - near_v[3] * near_q[3]
            )
            out_ref[level] = marine * (
                tracer + time_step * (-flux + diffusivity * laplace(tracer, near_q))
            )
        return pressure, pe, pw, pn, ps, zonal_sum + zonal_new, merid_sum + merid_new

    blank = jnp.zeros((height, breadth), jnp.float32)
    blank_col = jnp.zeros((height, 1), jnp.float32)
    blank_row = jnp.zeros((1, breadth), jnp.float32)
    carry = lax.fori_loop(
        0, levels, body, (blank, blank_col, blank_col, blank_row, blank_row, blank, blank)
    )
    um_ref[...] = carry[5] / levels
    vm_ref[...] = carry[6] / levels


def column_step(u, v, t, s, marine, coriolis, he, hw, hn, hs):
    levels, height, breadth = u.shape
    field = jax.ShapeDtypeStruct((levels, height, breadth), jnp.float32)
    plane = jax.ShapeDtypeStruct((height, breadth), jnp.float32)
    return pl.pallas_call(
        column_kernel,
        out_shape=(field, field, field, field, plane, plane),
        interpret=INTERPRET,
    )(u, v, t, s, marine, coriolis, he, hw, hn, hs)


def laplace(field, near):
    return near[0] + near[1] + near[2] + near[3] - 4.0 * field


def local(
    zonal_current,
    meridional_current,
    warmth_anomaly,
    brine_anomaly,
    marine_indicator,
    retained_tile_indicator,
    seabed_thickness,
    elevation_pivot_entry,
):
    level_fields, height, breadth = zonal_current.shape
    marine_snapshot = marine_indicator.astype(jnp.float32)
    kept = jnp.repeat(
        jnp.repeat(retained_tile_indicator.astype(jnp.float32), BLK, axis=0), BLK, axis=1
    )
    open_cells = marine_snapshot * kept
    column = seabed_thickness * open_cells

    raw = (zonal_current, meridional_current, warmth_anomaly, brine_anomaly)

    def edges(index_field, index_mask, plane):
        return jnp.concatenate(
            [item[index_field] * marine_snapshot[index_mask] for item in raw] + [plane[index_mask][None]],
            axis=0,
        )

    parity = jnp.concatenate(
        [
            -jnp.ones((2 * level_fields,), jnp.float32),
            jnp.ones((2 * level_fields + 1,), jnp.float32),
        ]
    )[:, None]
    halo_all = exchange(
        edges((slice(None), slice(None), 0), (slice(None), 0), column),
        edges((slice(None), slice(None), -1), (slice(None), -1), column),
        edges((slice(None), 0, slice(None)), (0, slice(None)), column),
        edges((slice(None), -1, slice(None)), (-1, slice(None)), column),
        parity,
    )
    halo_c = tuple(item[4 * level_fields] for item in halo_all)
    near_c = around(column, halo_c)

    total_rows = height * lax.axis_size("lat")
    rows_global = (lax.axis_index("lat") * height + jnp.arange(height)).astype(jnp.float32)
    coriolis = (2.0 * (rows_global + 0.5) / total_rows - 1.0)[:, None]
    zonal_next, merid_next, warm_next, brine_next, zonal_mean, merid_mean = column_step(
        zonal_current,
        meridional_current,
        warmth_anomaly,
        brine_anomaly,
        marine_snapshot,
        jnp.broadcast_to(coriolis, (height, breadth)),
        halo_all[0][..., None],
        halo_all[1][..., None],
        halo_all[2][:, None, :],
        halo_all[3][:, None, :],
    )
    tracers = [warm_next, brine_next]

    means = jnp.stack([zonal_mean, merid_mean], axis=0)
    halo_m = halos(means, -jnp.ones((2, 1), jnp.float32))
    near_m = around(means, halo_m)
    rhs = (
        -source_gain
        * open_cells
        * 0.5
        * (near_m[0][0] - near_m[1][0] + near_m[2][1] - near_m[3][1])
    )
    weights = [0.5 * (column + near_c[side]) for side in range(4)]
    diag = elevation_pivot_entry + weights[0] + weights[1] + weights[2] + weights[3]
    unit = jnp.ones((), jnp.float32)

    def apply(direction, halo_d):
        near_x = around(direction, halo_d)
        return open_cells * (
            diag * direction
            - weights[0] * near_x[0]
            - weights[1] * near_x[1]
            - weights[2] * near_x[2]
            - weights[3] * near_x[3]
        )

    solution = jnp.zeros_like(rhs)
    residual = rhs
    precond = residual / diag
    direction = precond
    image = apply(direction, halos(direction, unit))
    pair = allsum(jnp.sum(jnp.stack([residual * precond, direction * image]), axis=(1, 2)))
    product_now = pair[0]
    curvature = pair[1]
    for step in range(ITERS):
        alpha = product_now / curvature
        solution = solution + alpha * direction
        residual = residual - alpha * image
        if step + 1 < ITERS:
            precond = residual / diag
            image_z = apply(precond, halos(precond, unit))
            sums = allsum(
                jnp.sum(
                    jnp.stack(
                        [residual * precond, precond * image_z, precond * image, direction * image_z]
                    ),
                    axis=(1, 2),
                )
            )
            product_next = sums[0]
            beta = product_next / product_now
            curvature = sums[1] + beta * (sums[2] + sums[3]) + beta * beta * curvature
            direction = precond + beta * direction
            image = image_z + beta * image
            product_now = product_next
    return (zonal_next, merid_next, tracers[0], tracers[1], solution, residual)


def solution(mesh):
    in_specs = (
        P(None, "lat", "lon"),
        P(None, "lat", "lon"),
        P(None, "lat", "lon"),
        P(None, "lat", "lon"),
        P("lat", "lon"),
        P("lat", "lon"),
        P("lat", "lon"),
        P("lat", "lon"),
    )
    out_specs = (
        P(None, "lat", "lon"),
        P(None, "lat", "lon"),
        P(None, "lat", "lon"),
        P(None, "lat", "lon"),
        P("lat", "lon"),
        P("lat", "lon"),
    )
    return jax.shard_map(local, mesh=mesh, in_specs=in_specs, out_specs=out_specs, check_vma=False)
```

```python
import jax
import jax.numpy as jnp
from jax import lax
from jax.sharding import PartitionSpec as P
from jax.experimental import pallas as pl
from jax.experimental.pallas import tpu as pltpu

INTERPRET = False

BLK = 16
ITERS = 3


time_step = 0.1
viscosity = 0.2
diffusivity = 0.15
thermal = 0.2
haline = 0.8
source_gain = 8.0


def allsum(value):
    count = lax.axis_size("lon") * lax.axis_size("lat")
    spread = jnp.broadcast_to(value, (count,) + jnp.shape(value))
    gathered = lax.all_to_all(spread, ("lon", "lat"), 0, 0, tiled=True)
    return jnp.sum(gathered, axis=0)


def exchange(first_col, last_col, first_row, last_row, parity):
    lon_count = lax.axis_size("lon")
    lat_count = lax.axis_size("lat")
    east = lax.ppermute(first_col, "lon", [((i + 1) % lon_count, i) for i in range(lon_count)])
    west = lax.ppermute(last_col, "lon", [(i, (i + 1) % lon_count) for i in range(lon_count)])
    north = lax.ppermute(first_row, "lat", [(i + 1, i) for i in range(lat_count - 1)])
    south = lax.ppermute(last_row, "lat", [(i, i + 1) for i in range(lat_count - 1)])
    top = lat_count - 1
    mirror = lax.ppermute(
        last_row,
        ("lon", "lat"),
        [(i * lat_count + top, (lon_count - 1 - i) * lat_count + top) for i in range(lon_count)],
    )
    folded = parity * mirror[..., ::-1]
    north = jnp.where(lax.axis_index("lat") == top, folded, north)
    return east, west, north, south


def halos(cells, parity):
    return exchange(cells[..., :, 0], cells[..., :, -1], cells[..., 0, :], cells[..., -1, :], parity)


def around(cells, halo):
    east, west, north, south = halo
    return (
        jnp.concatenate([cells[..., :, 1:], east[..., None]], axis=-1),
        jnp.concatenate([west[..., None], cells[..., :, :-1]], axis=-1),
        jnp.concatenate([cells[..., 1:, :], north[..., None, :]], axis=-2),
        jnp.concatenate([south[..., None, :], cells[..., :-1, :]], axis=-2),
    )


def column_kernel(
    u_ref, v_ref, t_ref, s_ref, m_ref, f_ref, he_ref, hw_ref, hn_ref, hs_ref,
    un_ref, vn_ref, tn_ref, sn_ref, um_ref, vm_ref,
):
    levels, height, breadth = u_ref.shape
    marine = m_ref[...]
    coriolis = f_ref[...]
    row = lax.broadcasted_iota(jnp.int32, (height, breadth), 0)
    col = lax.broadcasted_iota(jnp.int32, (height, breadth), 1)
    last_row = row == height - 1
    first_row = row == 0
    last_col = col == breadth - 1
    first_col = col == 0

    def near(q, e, w, n, s):
        return (
            jnp.where(last_col, e, pltpu.roll(q, breadth - 1, 1)),
            jnp.where(first_col, w, pltpu.roll(q, 1, 1)),
            jnp.where(last_row, n, pltpu.roll(q, height - 1, 0)),
            jnp.where(first_row, s, pltpu.roll(q, 1, 0)),
        )

    def side(index):
        return (
            he_ref[:, index : index + 1],
            hw_ref[:, index : index + 1],
            hn_ref[index : index + 1, :],
            hs_ref[index : index + 1, :],
        )

    def body(level, carry):
        pressure, pe, pw, pn, ps, zonal_sum, merid_sum = carry
        zonal = u_ref[level] * marine
        merid = v_ref[level] * marine
        enthalpy_content = t_ref[level] * marine
        salt = s_ref[level] * marine
        halo_u = side(level)
        halo_v = side(levels + level)
        halo_t = side(2 * levels + level)
        halo_s = side(3 * levels + level)
        pressure = pressure + (haline * salt - thermal * enthalpy_content)
        pe = pe + (haline * halo_s[0] - thermal * halo_t[0])
        pw = pw + (haline * halo_s[1] - thermal * halo_t[1])
        pn = pn + (haline * halo_s[2] - thermal * halo_t[2])
        ps = ps + (haline * halo_s[3] - thermal * halo_t[3])
        near_p = near(pressure, pe, pw, pn, ps)
        near_u = near(zonal, *halo_u)
        near_v = near(merid, *halo_v)
        near_t = near(enthalpy_content, *halo_t)
        near_s = near(salt, *halo_s)
        zonal_new = marine * (
            zonal
            + time_step
            * (coriolis * merid - 0.5 * (near_p[0] - near_p[1]) + viscosity * laplace(zonal, near_u))
        )
        merid_new = marine * (
            merid
            + time_step
            * (-coriolis * zonal - 0.5 * (near_p[2] - near_p[3]) + viscosity * laplace(merid, near_v))
        )
        un_ref[level] = zonal_new
        vn_ref[level] = merid_new
        for tracer, near_q, out_ref in ((enthalpy_content, near_t, tn_ref), (salt, near_s, sn_ref)):
            flux = 0.5 * (
                near_u[0] * near_q[0]
                - near_u[1] * near_q[1]
                + near_v[2] * near_q[2]
                - near_v[3] * near_q[3]
            )
            out_ref[level] = marine * (
                tracer + time_step * (-flux + diffusivity * laplace(tracer, near_q))
            )
        return pressure, pe, pw, pn, ps, zonal_sum + zonal_new, merid_sum + merid_new

    blank = jnp.zeros((height, breadth), jnp.float32)
    blank_col = jnp.zeros((height, 1), jnp.float32)
    blank_row = jnp.zeros((1, breadth), jnp.float32)
    carry = (blank, blank_col, blank_col, blank_row, blank_row, blank, blank)
    for level in range(levels):
        carry = body(level, carry)
    um_ref[...] = carry[5] / levels
    vm_ref[...] = carry[6] / levels


def column_step(u, v, t, s, marine, coriolis, he, hw, hn, hs):
    levels, height, breadth = u.shape
    field = jax.ShapeDtypeStruct((levels, height, breadth), jnp.float32)
    plane = jax.ShapeDtypeStruct((height, breadth), jnp.float32)
    return pl.pallas_call(
        column_kernel,
        out_shape=(field, field, field, field, plane, plane),
        interpret=INTERPRET,
    )(u, v, t, s, marine, coriolis, he, hw, hn, hs)


def laplace(field, near):
    return near[0] + near[1] + near[2] + near[3] - 4.0 * field


def local(
    zonal_current,
    meridional_current,
    warmth_anomaly,
    brine_anomaly,
    marine_indicator,
    retained_tile_indicator,
    seabed_thickness,
    elevation_pivot_entry,
):
    level_fields, height, breadth = zonal_current.shape
    marine_snapshot = marine_indicator.astype(jnp.float32)
    kept = jnp.repeat(
        jnp.repeat(retained_tile_indicator.astype(jnp.float32), BLK, axis=0), BLK, axis=1
    )
    open_cells = marine_snapshot * kept
    column = seabed_thickness * open_cells

    raw = (zonal_current, meridional_current, warmth_anomaly, brine_anomaly)

    def row_edges(at):
        return jnp.concatenate(
            [item[:, at, :] * marine_snapshot[at] for item in raw] + [column[at][None]], axis=0
        )

    def col_edges(at):
        return jnp.concatenate(
            [(item[:, :, at] * marine_snapshot[:, at]).T for item in raw] + [column[:, at][:, None]],
            axis=1,
        )

    parity = jnp.concatenate(
        [
            -jnp.ones((2 * level_fields,), jnp.float32),
            jnp.ones((2 * level_fields + 1,), jnp.float32),
        ]
    )[:, None]
    halo_all = exchange(col_edges(0), col_edges(-1), row_edges(0), row_edges(-1), parity)
    halo_c = (
        halo_all[0][:, 4 * level_fields],
        halo_all[1][:, 4 * level_fields],
        halo_all[2][4 * level_fields],
        halo_all[3][4 * level_fields],
    )
    near_c = around(column, halo_c)

    total_rows = height * lax.axis_size("lat")
    rows_global = (lax.axis_index("lat") * height + jnp.arange(height)).astype(jnp.float32)
    coriolis = (2.0 * (rows_global + 0.5) / total_rows - 1.0)[:, None]
    zonal_next, merid_next, warm_next, brine_next, zonal_mean, merid_mean = column_step(
        zonal_current,
        meridional_current,
        warmth_anomaly,
        brine_anomaly,
        marine_snapshot,
        jnp.broadcast_to(coriolis, (height, breadth)),
        halo_all[0],
        halo_all[1],
        halo_all[2],
        halo_all[3],
    )
    tracers = [warm_next, brine_next]

    means = jnp.stack([zonal_mean, merid_mean], axis=0)
    halo_m = halos(means, -jnp.ones((2, 1), jnp.float32))
    near_m = around(means, halo_m)
    rhs = (
        -source_gain
        * open_cells
        * 0.5
        * (near_m[0][0] - near_m[1][0] + near_m[2][1] - near_m[3][1])
    )
    weights = [0.5 * (column + near_c[side]) for side in range(4)]
    diag = elevation_pivot_entry + weights[0] + weights[1] + weights[2] + weights[3]
    unit = jnp.ones((), jnp.float32)

    def apply(direction, halo_d):
        near_x = around(direction, halo_d)
        return open_cells * (
            diag * direction
            - weights[0] * near_x[0]
            - weights[1] * near_x[1]
            - weights[2] * near_x[2]
            - weights[3] * near_x[3]
        )

    solution = jnp.zeros_like(rhs)
    residual = rhs
    precond = residual / diag
    direction = precond
    image = apply(direction, halos(direction, unit))
    pair = allsum(jnp.sum(jnp.stack([residual * precond, direction * image]), axis=(1, 2)))
    product_now = pair[0]
    curvature = pair[1]
    for step in range(ITERS):
        alpha = product_now / curvature
        solution = solution + alpha * direction
        residual = residual - alpha * image
        if step + 1 < ITERS:
            precond = residual / diag
            image_z = apply(precond, halos(precond, unit))
            sums = allsum(
                jnp.sum(
                    jnp.stack(
                        [residual * precond, precond * image_z, precond * image, direction * image_z]
                    ),
                    axis=(1, 2),
                )
            )
            product_next = sums[0]
            beta = product_next / product_now
            curvature = sums[1] + beta * (sums[2] + sums[3]) + beta * beta * curvature
            direction = precond + beta * direction
            image = image_z + beta * image
            product_now = product_next
    return (zonal_next, merid_next, tracers[0], tracers[1], solution, residual)


def solution(mesh):
    in_specs = (
        P(None, "lat", "lon"),
        P(None, "lat", "lon"),
        P(None, "lat", "lon"),
        P(None, "lat", "lon"),
        P("lat", "lon"),
        P("lat", "lon"),
        P("lat", "lon"),
        P("lat", "lon"),
    )
    out_specs = (
        P(None, "lat", "lon"),
        P(None, "lat", "lon"),
        P(None, "lat", "lon"),
        P(None, "lat", "lon"),
        P("lat", "lon"),
        P("lat", "lon"),
    )
    return jax.shard_map(local, mesh=mesh, in_specs=in_specs, out_specs=out_specs, check_vma=False)
```

```python
import jax
import jax.numpy as jnp
from jax import lax
from jax.sharding import PartitionSpec as P
from jax.experimental import pallas as pl
from jax.experimental.pallas import tpu as pltpu

INTERPRET = False

BLK = 16
ITERS = 3


time_step = 0.1
viscosity = 0.2
diffusivity = 0.15
thermal = 0.2
haline = 0.8
source_gain = 8.0


def allsum(value):
    count = lax.axis_size("lon") * lax.axis_size("lat")
    spread = jnp.broadcast_to(value, (count,) + jnp.shape(value))
    gathered = lax.all_to_all(spread, ("lon", "lat"), 0, 0, tiled=True)
    return jnp.sum(gathered, axis=0)


def exchange(first_col, last_col, first_row, last_row, parity):
    lon_count = lax.axis_size("lon")
    lat_count = lax.axis_size("lat")
    east = lax.ppermute(first_col, "lon", [((i + 1) % lon_count, i) for i in range(lon_count)])
    west = lax.ppermute(last_col, "lon", [(i, (i + 1) % lon_count) for i in range(lon_count)])
    north = lax.ppermute(first_row, "lat", [(i + 1, i) for i in range(lat_count - 1)])
    south = lax.ppermute(last_row, "lat", [(i, i + 1) for i in range(lat_count - 1)])
    top = lat_count - 1
    mirror = lax.ppermute(
        last_row,
        ("lon", "lat"),
        [(i * lat_count + top, (lon_count - 1 - i) * lat_count + top) for i in range(lon_count)],
    )
    folded = parity * mirror[..., ::-1]
    north = jnp.where(lax.axis_index("lat") == top, folded, north)
    return east, west, north, south


def halos(cells, parity):
    return exchange(cells[..., :, 0], cells[..., :, -1], cells[..., 0, :], cells[..., -1, :], parity)


def around(cells, halo):
    east, west, north, south = halo
    return (
        jnp.concatenate([cells[..., :, 1:], east[..., None]], axis=-1),
        jnp.concatenate([west[..., None], cells[..., :, :-1]], axis=-1),
        jnp.concatenate([cells[..., 1:, :], north[..., None, :]], axis=-2),
        jnp.concatenate([south[..., None, :], cells[..., :-1, :]], axis=-2),
    )


def column_kernel(
    u_ref, v_ref, t_ref, s_ref, m_ref, f_ref, he_ref, hw_ref, hn_ref, hs_ref,
    un_ref, vn_ref, tn_ref, sn_ref, um_ref, vm_ref,
):
    levels, height, breadth = u_ref.shape
    marine = m_ref[...]
    coriolis = f_ref[...]
    row = lax.broadcasted_iota(jnp.int32, (height, breadth), 0)
    col = lax.broadcasted_iota(jnp.int32, (height, breadth), 1)
    last_row = row == height - 1
    first_row = row == 0
    last_col = col == breadth - 1
    first_col = col == 0

    def near(q, e, w, n, s):
        return (
            jnp.where(last_col, e, pltpu.roll(q, breadth - 1, 1)),
            jnp.where(first_col, w, pltpu.roll(q, 1, 1)),
            jnp.where(last_row, n, pltpu.roll(q, height - 1, 0)),
            jnp.where(first_row, s, pltpu.roll(q, 1, 0)),
        )

    def side(index):
        return (
            he_ref[:, index : index + 1],
            hw_ref[:, index : index + 1],
            hn_ref[index : index + 1, :],
            hs_ref[index : index + 1, :],
        )

    def body(level, carry):
        pressure, pe, pw, pn, ps, zonal_sum, merid_sum = carry
        zonal = u_ref[level] * marine
        merid = v_ref[level] * marine
        enthalpy_content = t_ref[level] * marine
        salt = s_ref[level] * marine
        halo_u = side(level)
        halo_v = side(levels + level)
        halo_t = side(2 * levels + level)
        halo_s = side(3 * levels + level)
        pressure = pressure + (haline * salt - thermal * enthalpy_content)
        pe = pe + (haline * halo_s[0] - thermal * halo_t[0])
        pw = pw + (haline * halo_s[1] - thermal * halo_t[1])
        pn = pn + (haline * halo_s[2] - thermal * halo_t[2])
        ps = ps + (haline * halo_s[3] - thermal * halo_t[3])
        near_p = near(pressure, pe, pw, pn, ps)
        near_u = near(zonal, *halo_u)
        near_v = near(merid, *halo_v)
        near_t = near(enthalpy_content, *halo_t)
        near_s = near(salt, *halo_s)
        zonal_new = marine * (
            zonal
            + time_step
            * (coriolis * merid - 0.5 * (near_p[0] - near_p[1]) + viscosity * laplace(zonal, near_u))
        )
        merid_new = marine * (
            merid
            + time_step
            * (-coriolis * zonal - 0.5 * (near_p[2] - near_p[3]) + viscosity * laplace(merid, near_v))
        )
        un_ref[level] = zonal_new
        vn_ref[level] = merid_new
        for tracer, near_q, out_ref in ((enthalpy_content, near_t, tn_ref), (salt, near_s, sn_ref)):
            flux = 0.5 * (
                near_u[0] * near_q[0]
                - near_u[1] * near_q[1]
                + near_v[2] * near_q[2]
                - near_v[3] * near_q[3]
            )
            out_ref[level] = marine * (
                tracer + time_step * (-flux + diffusivity * laplace(tracer, near_q))
            )
        return pressure, pe, pw, pn, ps, zonal_sum + zonal_new, merid_sum + merid_new

    blank = jnp.zeros((height, breadth), jnp.float32)
    blank_col = jnp.zeros((height, 1), jnp.float32)
    blank_row = jnp.zeros((1, breadth), jnp.float32)
    carry = (blank, blank_col, blank_col, blank_row, blank_row, blank, blank)
    for level in range(levels):
        carry = body(level, carry)
    um_ref[...] = carry[5] / levels
    vm_ref[...] = carry[6] / levels


def edge_kernel(u_ref, v_ref, t_ref, s_ref, m_ref, c_ref, cf_ref, cl_ref, rf_ref, rl_ref):
    levels, height, breadth = u_ref.shape
    marine = m_ref[...]
    lane = lax.broadcasted_iota(jnp.int32, cf_ref.shape, 1)
    first = jnp.zeros(cf_ref.shape, jnp.float32)
    last = jnp.zeros(cf_ref.shape, jnp.float32)
    rf_ref[...] = jnp.zeros(rf_ref.shape, jnp.float32)
    rl_ref[...] = jnp.zeros(rl_ref.shape, jnp.float32)
    planes = [(field, level) for field in (u_ref, v_ref, t_ref, s_ref) for level in range(levels)]
    for index, (field, level) in enumerate(planes + [(c_ref, None)]):
        if level is None:
            masked = field[...]
        else:
            masked = field[level] * marine
        first = jnp.where(lane == index, masked[:, 0:1], first)
        last = jnp.where(lane == index, masked[:, breadth - 1 : breadth], last)
        rf_ref[index : index + 1, :] = masked[0:1, :]
        rl_ref[index : index + 1, :] = masked[height - 1 : height, :]
    cf_ref[...] = first
    cl_ref[...] = last


def edge_step(u, v, t, s, marine, column):
    levels, height, breadth = u.shape
    count = 4 * levels + 1
    lanes = -(-count // 128) * 128
    rows = -(-count // 8) * 8
    cols = jax.ShapeDtypeStruct((height, lanes), jnp.float32)
    flat = jax.ShapeDtypeStruct((rows, breadth), jnp.float32)
    return pl.pallas_call(
        edge_kernel,
        out_shape=(cols, cols, flat, flat),
        interpret=INTERPRET,
    )(u, v, t, s, marine, column)


def column_step(u, v, t, s, marine, coriolis, he, hw, hn, hs):
    levels, height, breadth = u.shape
    field = jax.ShapeDtypeStruct((levels, height, breadth), jnp.float32)
    plane = jax.ShapeDtypeStruct((height, breadth), jnp.float32)
    return pl.pallas_call(
        column_kernel,
        out_shape=(field, field, field, field, plane, plane),
        interpret=INTERPRET,
    )(u, v, t, s, marine, coriolis, he, hw, hn, hs)


def laplace(field, near):
    return near[0] + near[1] + near[2] + near[3] - 4.0 * field


def local(
    zonal_current,
    meridional_current,
    warmth_anomaly,
    brine_anomaly,
    marine_indicator,
    retained_tile_indicator,
    seabed_thickness,
    elevation_pivot_entry,
):
    level_fields, height, breadth = zonal_current.shape
    marine_snapshot = marine_indicator.astype(jnp.float32)
    kept = jnp.repeat(
        jnp.repeat(retained_tile_indicator.astype(jnp.float32), BLK, axis=0), BLK, axis=1
    )
    open_cells = marine_snapshot * kept
    column = seabed_thickness * open_cells


    edge_cols_first, edge_cols_last, edge_rows_first, edge_rows_last = edge_step(
        zonal_current, meridional_current, warmth_anomaly, brine_anomaly, marine_snapshot, column
    )
    parity = jnp.where(
        jnp.arange(edge_rows_first.shape[0]) < 2 * level_fields, -1.0, 1.0
    ).astype(jnp.float32)[:, None]
    halo_all = exchange(edge_cols_first, edge_cols_last, edge_rows_first, edge_rows_last, parity)
    halo_c = (
        halo_all[0][:, 4 * level_fields],
        halo_all[1][:, 4 * level_fields],
        halo_all[2][4 * level_fields],
        halo_all[3][4 * level_fields],
    )
    near_c = around(column, halo_c)

    total_rows = height * lax.axis_size("lat")
    rows_global = (lax.axis_index("lat") * height + jnp.arange(height)).astype(jnp.float32)
    coriolis = (2.0 * (rows_global + 0.5) / total_rows - 1.0)[:, None]
    zonal_next, merid_next, warm_next, brine_next, zonal_mean, merid_mean = column_step(
        zonal_current,
        meridional_current,
        warmth_anomaly,
        brine_anomaly,
        marine_snapshot,
        jnp.broadcast_to(coriolis, (height, breadth)),
        halo_all[0],
        halo_all[1],
        halo_all[2],
        halo_all[3],
    )
    tracers = [warm_next, brine_next]

    means = jnp.stack([zonal_mean, merid_mean], axis=0)
    halo_m = halos(means, -jnp.ones((2, 1), jnp.float32))
    near_m = around(means, halo_m)
    rhs = (
        -source_gain
        * open_cells
        * 0.5
        * (near_m[0][0] - near_m[1][0] + near_m[2][1] - near_m[3][1])
    )
    weights = [0.5 * (column + near_c[side]) for side in range(4)]
    diag = elevation_pivot_entry + weights[0] + weights[1] + weights[2] + weights[3]
    unit = jnp.ones((), jnp.float32)

    def apply(direction, halo_d):
        near_x = around(direction, halo_d)
        return open_cells * (
            diag * direction
            - weights[0] * near_x[0]
            - weights[1] * near_x[1]
            - weights[2] * near_x[2]
            - weights[3] * near_x[3]
        )

    solution = jnp.zeros_like(rhs)
    residual = rhs
    precond = residual / diag
    direction = precond
    image = apply(direction, halos(direction, unit))
    pair = allsum(jnp.sum(jnp.stack([residual * precond, direction * image]), axis=(1, 2)))
    product_now = pair[0]
    curvature = pair[1]
    for step in range(ITERS):
        alpha = product_now / curvature
        solution = solution + alpha * direction
        residual = residual - alpha * image
        if step + 1 < ITERS:
            precond = residual / diag
            image_z = apply(precond, halos(precond, unit))
            sums = allsum(
                jnp.sum(
                    jnp.stack(
                        [residual * precond, precond * image_z, precond * image, direction * image_z]
                    ),
                    axis=(1, 2),
                )
            )
            product_next = sums[0]
            beta = product_next / product_now
            curvature = sums[1] + beta * (sums[2] + sums[3]) + beta * beta * curvature
            direction = precond + beta * direction
            image = image_z + beta * image
            product_now = product_next
    return (zonal_next, merid_next, tracers[0], tracers[1], solution, residual)


def solution(mesh):
    in_specs = (
        P(None, "lat", "lon"),
        P(None, "lat", "lon"),
        P(None, "lat", "lon"),
        P(None, "lat", "lon"),
        P("lat", "lon"),
        P("lat", "lon"),
        P("lat", "lon"),
        P("lat", "lon"),
    )
    out_specs = (
        P(None, "lat", "lon"),
        P(None, "lat", "lon"),
        P(None, "lat", "lon"),
        P(None, "lat", "lon"),
        P("lat", "lon"),
        P("lat", "lon"),
    )
    return jax.shard_map(local, mesh=mesh, in_specs=in_specs, out_specs=out_specs, check_vma=False)
```

```python
import jax
import jax.numpy as jnp
from jax import lax
from jax.sharding import PartitionSpec as P
from jax.experimental import pallas as pl
from jax.experimental.pallas import tpu as pltpu

INTERPRET = False

BLK = 16
ITERS = 3


time_step = 0.1
viscosity = 0.2
diffusivity = 0.15
thermal = 0.2
haline = 0.8
source_gain = 8.0


def allsum(value):
    count = lax.axis_size("lon") * lax.axis_size("lat")
    spread = jnp.broadcast_to(value, (count,) + jnp.shape(value))
    gathered = lax.all_to_all(spread, ("lon", "lat"), 0, 0, tiled=True)
    return jnp.sum(gathered, axis=0)


def exchange(first_col, last_col, first_row, last_row, parity):
    lon_count = lax.axis_size("lon")
    lat_count = lax.axis_size("lat")
    east = lax.ppermute(first_col, "lon", [((i + 1) % lon_count, i) for i in range(lon_count)])
    west = lax.ppermute(last_col, "lon", [(i, (i + 1) % lon_count) for i in range(lon_count)])
    north = lax.ppermute(first_row, "lat", [(i + 1, i) for i in range(lat_count - 1)])
    south = lax.ppermute(last_row, "lat", [(i, i + 1) for i in range(lat_count - 1)])
    top = lat_count - 1
    mirror = lax.ppermute(
        last_row,
        ("lon", "lat"),
        [(i * lat_count + top, (lon_count - 1 - i) * lat_count + top) for i in range(lon_count)],
    )
    folded = parity * mirror[..., ::-1]
    north = jnp.where(lax.axis_index("lat") == top, folded, north)
    return east, west, north, south


def halos(cells, parity):
    return exchange(cells[..., :, 0], cells[..., :, -1], cells[..., 0, :], cells[..., -1, :], parity)


def around(cells, halo):
    east, west, north, south = halo
    return (
        jnp.concatenate([cells[..., :, 1:], east[..., None]], axis=-1),
        jnp.concatenate([west[..., None], cells[..., :, :-1]], axis=-1),
        jnp.concatenate([cells[..., 1:, :], north[..., None, :]], axis=-2),
        jnp.concatenate([south[..., None, :], cells[..., :-1, :]], axis=-2),
    )


def column_kernel(
    u_ref, v_ref, t_ref, s_ref, m_ref, f_ref, he_ref, hw_ref, hn_ref, hs_ref,
    un_ref, vn_ref, tn_ref, sn_ref, um_ref, vm_ref,
):
    levels, height, breadth = u_ref.shape
    marine = m_ref[...]
    coriolis = f_ref[...]
    row = lax.broadcasted_iota(jnp.int32, (height, breadth), 0)
    col = lax.broadcasted_iota(jnp.int32, (height, breadth), 1)
    last_row = row == height - 1
    first_row = row == 0
    last_col = col == breadth - 1
    first_col = col == 0

    def near(q, e, w, n, s):
        return (
            jnp.where(last_col, e, pltpu.roll(q, breadth - 1, 1)),
            jnp.where(first_col, w, pltpu.roll(q, 1, 1)),
            jnp.where(last_row, n, pltpu.roll(q, height - 1, 0)),
            jnp.where(first_row, s, pltpu.roll(q, 1, 0)),
        )

    def side(index):
        return (
            he_ref[:, index : index + 1],
            hw_ref[:, index : index + 1],
            hn_ref[index : index + 1, :],
            hs_ref[index : index + 1, :],
        )

    def body(level, carry):
        pressure, pe, pw, pn, ps, zonal_sum, merid_sum = carry
        zonal = u_ref[level] * marine
        merid = v_ref[level] * marine
        enthalpy_content = t_ref[level] * marine
        salt = s_ref[level] * marine
        halo_u = side(level)
        halo_v = side(levels + level)
        halo_t = side(2 * levels + level)
        halo_s = side(3 * levels + level)
        pressure = pressure + (haline * salt - thermal * enthalpy_content)
        pe = pe + (haline * halo_s[0] - thermal * halo_t[0])
        pw = pw + (haline * halo_s[1] - thermal * halo_t[1])
        pn = pn + (haline * halo_s[2] - thermal * halo_t[2])
        ps = ps + (haline * halo_s[3] - thermal * halo_t[3])
        near_p = near(pressure, pe, pw, pn, ps)
        near_u = near(zonal, *halo_u)
        near_v = near(merid, *halo_v)
        near_t = near(enthalpy_content, *halo_t)
        near_s = near(salt, *halo_s)
        zonal_new = marine * (
            zonal
            + time_step
            * (coriolis * merid - 0.5 * (near_p[0] - near_p[1]) + viscosity * laplace(zonal, near_u))
        )
        merid_new = marine * (
            merid
            + time_step
            * (-coriolis * zonal - 0.5 * (near_p[2] - near_p[3]) + viscosity * laplace(merid, near_v))
        )
        un_ref[level] = zonal_new
        vn_ref[level] = merid_new
        for tracer, near_q, out_ref in ((enthalpy_content, near_t, tn_ref), (salt, near_s, sn_ref)):
            flux = 0.5 * (
                near_u[0] * near_q[0]
                - near_u[1] * near_q[1]
                + near_v[2] * near_q[2]
                - near_v[3] * near_q[3]
            )
            out_ref[level] = marine * (
                tracer + time_step * (-flux + diffusivity * laplace(tracer, near_q))
            )
        return pressure, pe, pw, pn, ps, zonal_sum + zonal_new, merid_sum + merid_new

    blank = jnp.zeros((height, breadth), jnp.float32)
    blank_col = jnp.zeros((height, 1), jnp.float32)
    blank_row = jnp.zeros((1, breadth), jnp.float32)
    carry = (blank, blank_col, blank_col, blank_row, blank_row, blank, blank)
    for level in range(levels):
        carry = body(level, carry)
    um_ref[...] = carry[5] / levels
    vm_ref[...] = carry[6] / levels


def edge_kernel(u_ref, v_ref, t_ref, s_ref, m_ref, c_ref, cf_ref, cl_ref, rf_ref, rl_ref):
    levels, height, breadth = u_ref.shape
    marine = m_ref[...]
    lane = lax.broadcasted_iota(jnp.int32, cf_ref.shape, 1)
    first = jnp.zeros(cf_ref.shape, jnp.float32)
    last = jnp.zeros(cf_ref.shape, jnp.float32)
    rf_ref[...] = jnp.zeros(rf_ref.shape, jnp.float32)
    rl_ref[...] = jnp.zeros(rl_ref.shape, jnp.float32)
    planes = [(field, level) for field in (u_ref, v_ref, t_ref, s_ref) for level in range(levels)]
    for index, (field, level) in enumerate(planes + [(c_ref, None)]):
        if level is None:
            masked = field[...]
        else:
            masked = field[level] * marine
        first = jnp.where(lane == index, masked[:, 0:1], first)
        last = jnp.where(lane == index, masked[:, breadth - 1 : breadth], last)
        rf_ref[index : index + 1, :] = masked[0:1, :]
        rl_ref[index : index + 1, :] = masked[height - 1 : height, :]
    cf_ref[...] = first
    cl_ref[...] = last


def edge_step(u, v, t, s, marine, column):
    levels, height, breadth = u.shape
    count = 4 * levels + 1
    lanes = -(-count // 128) * 128
    rows = -(-count // 8) * 8
    cols = jax.ShapeDtypeStruct((height, lanes), jnp.float32)
    flat = jax.ShapeDtypeStruct((rows, breadth), jnp.float32)
    return pl.pallas_call(
        edge_kernel,
        out_shape=(cols, cols, flat, flat),
        interpret=INTERPRET,
    )(u, v, t, s, marine, column)


def column_step(u, v, t, s, marine, coriolis, he, hw, hn, hs):
    levels, height, breadth = u.shape
    field = jax.ShapeDtypeStruct((levels, height, breadth), jnp.float32)
    plane = jax.ShapeDtypeStruct((height, breadth), jnp.float32)
    return pl.pallas_call(
        column_kernel,
        out_shape=(field, field, field, field, plane, plane),
        interpret=INTERPRET,
    )(u, v, t, s, marine, coriolis, he, hw, hn, hs)


def laplace(field, near):
    return near[0] + near[1] + near[2] + near[3] - 4.0 * field


def local(
    zonal_current,
    meridional_current,
    warmth_anomaly,
    brine_anomaly,
    marine_indicator,
    retained_tile_indicator,
    seabed_thickness,
    elevation_pivot_entry,
):
    level_fields, height, breadth = zonal_current.shape
    marine_snapshot = marine_indicator.astype(jnp.float32)
    kept = jnp.repeat(
        jnp.repeat(retained_tile_indicator.astype(jnp.float32), BLK, axis=0), BLK, axis=1
    )
    open_cells = marine_snapshot * kept
    column = seabed_thickness * open_cells


    edge_cols_first, edge_cols_last, edge_rows_first, edge_rows_last = edge_step(
        zonal_current, meridional_current, warmth_anomaly, brine_anomaly, marine_snapshot, column
    )
    parity = jnp.where(
        jnp.arange(edge_rows_first.shape[0]) < 2 * level_fields, -1.0, 1.0
    ).astype(jnp.float32)[:, None]
    halo_all = exchange(edge_cols_first, edge_cols_last, edge_rows_first, edge_rows_last, parity)
    halo_c = (
        halo_all[0][:, 4 * level_fields],
        halo_all[1][:, 4 * level_fields],
        halo_all[2][4 * level_fields],
        halo_all[3][4 * level_fields],
    )
    near_c = around(column, halo_c)

    total_rows = height * lax.axis_size("lat")
    rows_global = (lax.axis_index("lat") * height + jnp.arange(height)).astype(jnp.float32)
    coriolis = (2.0 * (rows_global + 0.5) / total_rows - 1.0)[:, None]
    zonal_next, merid_next, warm_next, brine_next, zonal_mean, merid_mean = column_step(
        zonal_current,
        meridional_current,
        warmth_anomaly,
        brine_anomaly,
        marine_snapshot,
        jnp.broadcast_to(coriolis, (height, breadth)),
        halo_all[0],
        halo_all[1],
        halo_all[2],
        halo_all[3],
    )
    tracers = [warm_next, brine_next]

    means = jnp.stack([zonal_mean, merid_mean], axis=0)
    halo_m = halos(means, -jnp.ones((2, 1), jnp.float32))
    near_m = around(means, halo_m)
    rhs = (
        -source_gain
        * open_cells
        * 0.5
        * (near_m[0][0] - near_m[1][0] + near_m[2][1] - near_m[3][1])
    )
    weights = [0.5 * (column + near_c[side]) for side in range(4)]
    diag = elevation_pivot_entry + weights[0] + weights[1] + weights[2] + weights[3]
    unit = jnp.ones((), jnp.float32)

    def apply(direction, halo_d):
        near_x = around(direction, halo_d)
        return open_cells * (
            diag * direction
            - weights[0] * near_x[0]
            - weights[1] * near_x[1]
            - weights[2] * near_x[2]
            - weights[3] * near_x[3]
        )

    basis_v0 = rhs / diag
    basis_w1 = apply(basis_v0, halos(basis_v0, unit))
    basis_v1 = basis_w1 / diag
    basis_w2 = apply(basis_v1, halos(basis_v1, unit))
    gram = allsum(
        jnp.sum(
            jnp.stack(
                [
                    basis_v0 * rhs,
                    basis_v0 * basis_w1,
                    basis_v0 * basis_w2,
                    basis_v1 * rhs,
                    basis_v1 * basis_w1,
                    basis_v1 * basis_w2,
                ]
            ),
            axis=(1, 2),
        )
    )
    product_now = gram[0]
    alpha = product_now / gram[1]
    solution = alpha * basis_v0
    residual = rhs - alpha * basis_w1
    direction = basis_v0
    image = basis_w1
    if ITERS > 1:
        shift = -alpha
        product_next = gram[0] + shift * (gram[1] + gram[3]) + shift * shift * gram[4]
        beta = product_next / product_now
        first = 1.0 + beta
        curvature = (
            first * first * gram[1]
            + first * shift * (gram[2] + gram[4])
            + shift * shift * gram[5]
        )
        product_now = product_next
        alpha = product_now / curvature
        direction = first * basis_v0 + shift * basis_v1
        image = first * basis_w1 + shift * basis_w2
        solution = solution + alpha * direction
        residual = rhs + (shift - alpha * first) * basis_w1 - (alpha * shift) * basis_w2
    for step in range(2, ITERS):
        precond = residual / diag
        image_z = apply(precond, halos(precond, unit))
        sums = allsum(
            jnp.sum(
                jnp.stack(
                    [
                        residual * precond,
                        precond * image_z,
                        precond * image,
                        direction * image_z,
                        direction * image,
                    ]
                ),
                axis=(1, 2),
            )
        )
        product_next = sums[0]
        beta = product_next / product_now
        curvature = sums[1] + beta * (sums[2] + sums[3]) + beta * beta * sums[4]
        direction = precond + beta * direction
        image = image_z + beta * image
        product_now = product_next
        alpha = product_now / curvature
        solution = solution + alpha * direction
        residual = residual - alpha * image
    return (zonal_next, merid_next, tracers[0], tracers[1], solution, residual)


def solution(mesh):
    in_specs = (
        P(None, "lat", "lon"),
        P(None, "lat", "lon"),
        P(None, "lat", "lon"),
        P(None, "lat", "lon"),
        P("lat", "lon"),
        P("lat", "lon"),
        P("lat", "lon"),
        P("lat", "lon"),
    )
    out_specs = (
        P(None, "lat", "lon"),
        P(None, "lat", "lon"),
        P(None, "lat", "lon"),
        P(None, "lat", "lon"),
        P("lat", "lon"),
        P("lat", "lon"),
    )
    return jax.shard_map(local, mesh=mesh, in_specs=in_specs, out_specs=out_specs, check_vma=False)
```

```python
import jax
import jax.numpy as jnp
from jax import lax
from jax.sharding import PartitionSpec as P
from jax.experimental import pallas as pl
from jax.experimental.pallas import tpu as pltpu

INTERPRET = False

BLK = 16
ITERS = 3


time_step = 0.1
viscosity = 0.2
diffusivity = 0.15
thermal = 0.2
haline = 0.8
source_gain = 8.0


def allsum(value):
    count = lax.axis_size("lon") * lax.axis_size("lat")
    spread = jnp.broadcast_to(value, (count,) + jnp.shape(value))
    gathered = lax.all_to_all(spread, ("lon", "lat"), 0, 0, tiled=True)
    return jnp.sum(gathered, axis=0)


def exchange(first_col, last_col, first_row, last_row, parity):
    lon_count = lax.axis_size("lon")
    lat_count = lax.axis_size("lat")
    east = lax.ppermute(first_col, "lon", [((i + 1) % lon_count, i) for i in range(lon_count)])
    west = lax.ppermute(last_col, "lon", [(i, (i + 1) % lon_count) for i in range(lon_count)])
    north = lax.ppermute(first_row, "lat", [(i + 1, i) for i in range(lat_count - 1)])
    south = lax.ppermute(last_row, "lat", [(i, i + 1) for i in range(lat_count - 1)])
    top = lat_count - 1
    mirror = lax.ppermute(
        last_row,
        ("lon", "lat"),
        [(i * lat_count + top, (lon_count - 1 - i) * lat_count + top) for i in range(lon_count)],
    )
    folded = parity * mirror[..., ::-1]
    north = jnp.where(lax.axis_index("lat") == top, folded, north)
    return east, west, north, south


def halos(cells, parity):
    return exchange(cells[..., :, 0], cells[..., :, -1], cells[..., 0, :], cells[..., -1, :], parity)


def around(cells, halo):
    east, west, north, south = halo
    return (
        jnp.concatenate([cells[..., :, 1:], east[..., None]], axis=-1),
        jnp.concatenate([west[..., None], cells[..., :, :-1]], axis=-1),
        jnp.concatenate([cells[..., 1:, :], north[..., None, :]], axis=-2),
        jnp.concatenate([south[..., None, :], cells[..., :-1, :]], axis=-2),
    )


def column_kernel(
    u_ref, v_ref, t_ref, s_ref, m_ref, f_ref, he_ref, hw_ref, hn_ref, hs_ref,
    un_ref, vn_ref, tn_ref, sn_ref, um_ref, vm_ref,
):
    levels, height, breadth = u_ref.shape
    marine = m_ref[...]
    coriolis = f_ref[...]
    row = lax.broadcasted_iota(jnp.int32, (height, breadth), 0)
    col = lax.broadcasted_iota(jnp.int32, (height, breadth), 1)
    last_row = row == height - 1
    first_row = row == 0
    last_col = col == breadth - 1
    first_col = col == 0

    def near(q, e, w, n, s):
        return (
            jnp.where(last_col, e, pltpu.roll(q, breadth - 1, 1)),
            jnp.where(first_col, w, pltpu.roll(q, 1, 1)),
            jnp.where(last_row, n, pltpu.roll(q, height - 1, 0)),
            jnp.where(first_row, s, pltpu.roll(q, 1, 0)),
        )

    def side(index):
        return (
            he_ref[:, index : index + 1],
            hw_ref[:, index : index + 1],
            hn_ref[index : index + 1, :],
            hs_ref[index : index + 1, :],
        )

    def body(level, carry):
        pressure, pe, pw, pn, ps, zonal_sum, merid_sum = carry
        zonal = u_ref[level] * marine
        merid = v_ref[level] * marine
        enthalpy_content = t_ref[level] * marine
        salt = s_ref[level] * marine
        halo_u = side(level)
        halo_v = side(levels + level)
        halo_t = side(2 * levels + level)
        halo_s = side(3 * levels + level)
        pressure = pressure + (haline * salt - thermal * enthalpy_content)
        pe = pe + (haline * halo_s[0] - thermal * halo_t[0])
        pw = pw + (haline * halo_s[1] - thermal * halo_t[1])
        pn = pn + (haline * halo_s[2] - thermal * halo_t[2])
        ps = ps + (haline * halo_s[3] - thermal * halo_t[3])
        near_p = near(pressure, pe, pw, pn, ps)
        near_u = near(zonal, *halo_u)
        near_v = near(merid, *halo_v)
        near_t = near(enthalpy_content, *halo_t)
        near_s = near(salt, *halo_s)
        zonal_new = marine * (
            zonal
            + time_step
            * (coriolis * merid - 0.5 * (near_p[0] - near_p[1]) + viscosity * laplace(zonal, near_u))
        )
        merid_new = marine * (
            merid
            + time_step
            * (-coriolis * zonal - 0.5 * (near_p[2] - near_p[3]) + viscosity * laplace(merid, near_v))
        )
        un_ref[level] = zonal_new
        vn_ref[level] = merid_new
        for tracer, near_q, out_ref in ((enthalpy_content, near_t, tn_ref), (salt, near_s, sn_ref)):
            flux = 0.5 * (
                near_u[0] * near_q[0]
                - near_u[1] * near_q[1]
                + near_v[2] * near_q[2]
                - near_v[3] * near_q[3]
            )
            out_ref[level] = marine * (
                tracer + time_step * (-flux + diffusivity * laplace(tracer, near_q))
            )
        return pressure, pe, pw, pn, ps, zonal_sum + zonal_new, merid_sum + merid_new

    blank = jnp.zeros((height, breadth), jnp.float32)
    blank_col = jnp.zeros((height, 1), jnp.float32)
    blank_row = jnp.zeros((1, breadth), jnp.float32)
    carry = (blank, blank_col, blank_col, blank_row, blank_row, blank, blank)
    for level in range(levels):
        carry = body(level, carry)
    um_ref[...] = carry[5] / levels
    vm_ref[...] = carry[6] / levels


def edge_kernel(u_ref, v_ref, t_ref, s_ref, m_ref, c_ref, cf_ref, cl_ref, rf_ref, rl_ref):
    levels, height, breadth = u_ref.shape
    marine = m_ref[...]
    groups = cf_ref.shape[1] // 128
    lane = lax.broadcasted_iota(jnp.int32, (height, 128), 1)
    first = [jnp.zeros((height, 128), jnp.float32) for _ in range(groups)]
    last = [jnp.zeros((height, 128), jnp.float32) for _ in range(groups)]
    rf_ref[...] = jnp.zeros(rf_ref.shape, jnp.float32)
    rl_ref[...] = jnp.zeros(rl_ref.shape, jnp.float32)
    planes = [(field, level) for field in (u_ref, v_ref, t_ref, s_ref) for level in range(levels)]
    for index, (field, level) in enumerate(planes + [(c_ref, None)]):
        if level is None:
            masked = field[...]
        else:
            masked = field[level] * marine
        group, offset = divmod(index, 128)
        first[group] = jnp.where(lane == offset, masked[:, 0:1], first[group])
        last[group] = jnp.where(lane == offset, masked[:, breadth - 1 : breadth], last[group])
        rf_ref[index : index + 1, :] = masked[0:1, :]
        rl_ref[index : index + 1, :] = masked[height - 1 : height, :]
    for group in range(groups):
        cf_ref[:, group * 128 : (group + 1) * 128] = first[group]
        cl_ref[:, group * 128 : (group + 1) * 128] = last[group]


def edge_step(u, v, t, s, marine, column):
    levels, height, breadth = u.shape
    count = 4 * levels + 1
    lanes = -(-count // 128) * 128
    rows = -(-count // 8) * 8
    cols = jax.ShapeDtypeStruct((height, lanes), jnp.float32)
    flat = jax.ShapeDtypeStruct((rows, breadth), jnp.float32)
    return pl.pallas_call(
        edge_kernel,
        out_shape=(cols, cols, flat, flat),
        interpret=INTERPRET,
    )(u, v, t, s, marine, column)


def column_step(u, v, t, s, marine, coriolis, he, hw, hn, hs):
    levels, height, breadth = u.shape
    field = jax.ShapeDtypeStruct((levels, height, breadth), jnp.float32)
    plane = jax.ShapeDtypeStruct((height, breadth), jnp.float32)
    return pl.pallas_call(
        column_kernel,
        out_shape=(field, field, field, field, plane, plane),
        interpret=INTERPRET,
    )(u, v, t, s, marine, coriolis, he, hw, hn, hs)


def laplace(field, near):
    return near[0] + near[1] + near[2] + near[3] - 4.0 * field


def local(
    zonal_current,
    meridional_current,
    warmth_anomaly,
    brine_anomaly,
    marine_indicator,
    retained_tile_indicator,
    seabed_thickness,
    elevation_pivot_entry,
):
    level_fields, height, breadth = zonal_current.shape
    marine_snapshot = marine_indicator.astype(jnp.float32)
    kept = jnp.repeat(
        jnp.repeat(retained_tile_indicator.astype(jnp.float32), BLK, axis=0), BLK, axis=1
    )
    open_cells = marine_snapshot * kept
    column = seabed_thickness * open_cells


    edge_cols_first, edge_cols_last, edge_rows_first, edge_rows_last = edge_step(
        zonal_current, meridional_current, warmth_anomaly, brine_anomaly, marine_snapshot, column
    )
    parity = jnp.where(
        jnp.arange(edge_rows_first.shape[0]) < 2 * level_fields, -1.0, 1.0
    ).astype(jnp.float32)[:, None]
    halo_all = exchange(edge_cols_first, edge_cols_last, edge_rows_first, edge_rows_last, parity)
    halo_c = (
        halo_all[0][:, 4 * level_fields],
        halo_all[1][:, 4 * level_fields],
        halo_all[2][4 * level_fields],
        halo_all[3][4 * level_fields],
    )
    near_c = around(column, halo_c)

    total_rows = height * lax.axis_size("lat")
    rows_global = (lax.axis_index("lat") * height + jnp.arange(height)).astype(jnp.float32)
    coriolis = (2.0 * (rows_global + 0.5) / total_rows - 1.0)[:, None]
    zonal_next, merid_next, warm_next, brine_next, zonal_mean, merid_mean = column_step(
        zonal_current,
        meridional_current,
        warmth_anomaly,
        brine_anomaly,
        marine_snapshot,
        jnp.broadcast_to(coriolis, (height, breadth)),
        halo_all[0],
        halo_all[1],
        halo_all[2],
        halo_all[3],
    )
    tracers = [warm_next, brine_next]

    means = jnp.stack([zonal_mean, merid_mean], axis=0)
    halo_m = halos(means, -jnp.ones((2, 1), jnp.float32))
    near_m = around(means, halo_m)
    rhs = (
        -source_gain
        * open_cells
        * 0.5
        * (near_m[0][0] - near_m[1][0] + near_m[2][1] - near_m[3][1])
    )
    weights = [0.5 * (column + near_c[side]) for side in range(4)]
    diag = elevation_pivot_entry + weights[0] + weights[1] + weights[2] + weights[3]
    unit = jnp.ones((), jnp.float32)

    def apply(direction, halo_d):
        near_x = around(direction, halo_d)
        return open_cells * (
            diag * direction
            - weights[0] * near_x[0]
            - weights[1] * near_x[1]
            - weights[2] * near_x[2]
            - weights[3] * near_x[3]
        )

    basis_v0 = rhs / diag
    basis_w1 = apply(basis_v0, halos(basis_v0, unit))
    basis_v1 = basis_w1 / diag
    basis_w2 = apply(basis_v1, halos(basis_v1, unit))
    gram = allsum(
        jnp.sum(
            jnp.stack(
                [
                    basis_v0 * rhs,
                    basis_v0 * basis_w1,
                    basis_v0 * basis_w2,
                    basis_v1 * rhs,
                    basis_v1 * basis_w1,
                    basis_v1 * basis_w2,
                ]
            ),
            axis=(1, 2),
        )
    )
    product_now = gram[0]
    alpha = product_now / gram[1]
    solution = alpha * basis_v0
    residual = rhs - alpha * basis_w1
    direction = basis_v0
    image = basis_w1
    if ITERS > 1:
        shift = -alpha
        product_next = gram[0] + shift * (gram[1] + gram[3]) + shift * shift * gram[4]
        beta = product_next / product_now
        first = 1.0 + beta
        curvature = (
            first * first * gram[1]
            + first * shift * (gram[2] + gram[4])
            + shift * shift * gram[5]
        )
        product_now = product_next
        alpha = product_now / curvature
        direction = first * basis_v0 + shift * basis_v1
        image = first * basis_w1 + shift * basis_w2
        solution = solution + alpha * direction
        residual = rhs + (shift - alpha * first) * basis_w1 - (alpha * shift) * basis_w2
    for step in range(2, ITERS):
        precond = residual / diag
        image_z = apply(precond, halos(precond, unit))
        sums = allsum(
            jnp.sum(
                jnp.stack(
                    [
                        residual * precond,
                        precond * image_z,
                        precond * image,
                        direction * image_z,
                        direction * image,
                    ]
                ),
                axis=(1, 2),
            )
        )
        product_next = sums[0]
        beta = product_next / product_now
        curvature = sums[1] + beta * (sums[2] + sums[3]) + beta * beta * sums[4]
        direction = precond + beta * direction
        image = image_z + beta * image
        product_now = product_next
        alpha = product_now / curvature
        solution = solution + alpha * direction
        residual = residual - alpha * image
    return (zonal_next, merid_next, tracers[0], tracers[1], solution, residual)


def solution(mesh):
    in_specs = (
        P(None, "lat", "lon"),
        P(None, "lat", "lon"),
        P(None, "lat", "lon"),
        P(None, "lat", "lon"),
        P("lat", "lon"),
        P("lat", "lon"),
        P("lat", "lon"),
        P("lat", "lon"),
    )
    out_specs = (
        P(None, "lat", "lon"),
        P(None, "lat", "lon"),
        P(None, "lat", "lon"),
        P(None, "lat", "lon"),
        P("lat", "lon"),
        P("lat", "lon"),
    )
    return jax.shard_map(local, mesh=mesh, in_specs=in_specs, out_specs=out_specs, check_vma=False)
```
